32 devices in a mesh: dp: 2 (over x), seq: 8 (over z, y), tensor: 2 (over core).
Axes of the slice: x: 2, y: 2, z: 4, core: 2. Of those that a mesh axis runs over, the one named last changes fastest.
Arguments:
- queries: bfloat16 [2, 1024, 1536], P('dp', 'seq', 'tensor')
- keys: bfloat16 [2, 1024, 1536], P('dp', 'seq', 'tensor')
- values: bfloat16 [2, 1024, 1536], P('dp', 'seq', 'tensor'), may hold values from -6 to 6
- out_weight: bfloat16 [1536, 1536], P('tensor'), may hold values from -0.15625 to 0.15625
- residual: bfloat16 [2, 1024, 1536], P('dp', 'seq', 'tensor'), may hold values from -1.1953125 to 1.1953125
- lengths: int32 [2], P('dp'), may hold values from 512 to 1024
- grad_out: bfloat16 [2, 1024, 1536], P('dp', 'seq', 'tensor'), may hold values from -6 to 6
Outputs:
- block_out: bfloat16 [2, 1024, 1536], P('dp', 'seq', 'tensor')
- grad_queries: bfloat16 [2, 1024, 1536], P('dp', 'seq', 'tensor')
- grad_keys: bfloat16 [2, 1024, 1536], P('dp', 'seq', 'tensor')
- grad_values: bfloat16 [2, 1024, 1536], P('dp', 'seq', 'tensor')
- grad_weight: float32 [1536, 1536], P('tensor', ('dp', 'seq'))
The draws below stay inside these ranges and needn't reach their ends.
Inputs may be any that keep to these rules, and one draw needn't show every extreme that they name: Frames at positions from lengths[b] on are padding.
All inputs are finite; a program needn't handle non-finite values.
Results may differ from the reference program's by a relative error of at most 0.014.
Values may be sent and summed in bfloat16 or wider, within the bound.
No kernel may reach another device: no remote copies, remote signals or barrier semaphores. Data moves between devices by JAX's collectives and lax.ppermute only.
A program may use at most 64 MiB of HBM per device.

```python
import math
import jax
import jax.numpy as jnp
from jax import lax

D = 1536
HEADS = 16
HEAD_DIM = 96
FRAMES = 1024
BATCH = 2


def draw_keys(key, part):
    result = 1.5 * jax.random.normal(jax.random.fold_in(key, 11), (BATCH, FRAMES, D), jnp.float32)
    return result.astype(jnp.bfloat16)


def draw_queries(key, part):
    result = 1.5 * jax.random.normal(jax.random.fold_in(key, 21), (BATCH, FRAMES, D), jnp.float32)
    return result.astype(jnp.bfloat16)


def with_spikes(drawn, key, source, target, blocks, factor):
    def block_of(position):
        return (jnp.arange(drawn.shape[position]) // (drawn.shape[position] // blocks)).reshape((-1,) + (1,) * (drawn.ndim - 1 - position))

    first = jax.random.permutation(key, blocks)[block_of(target)]
    far = (block_of(target) + blocks // 2) % blocks
    return jnp.where((block_of(source) == first) | (block_of(source) == far), factor * drawn, drawn)


def block_levels(own_key, extent, shards, least, top_value):
    gain = 1.0
    for position, shards_of in shards:
        steps = jax.random.uniform(jax.random.fold_in(jax.random.fold_in(own_key, 6), position), (shards_of,), jnp.float32, least / len(shards), top_value / len(shards))
        gain = gain * jnp.repeat(jnp.exp(steps), extent[position] // shards_of).reshape((-1,) + (1,) * (len(extent) - 1 - position))
    return gain


def noise(stream_key, dims, scale, limit, split=(), kind=jnp.bfloat16):
    level = block_levels(stream_key, dims, split, -0.22, 0.18) if split else 1.0
    drawn = jax.random.normal(stream_key, dims, jnp.float32) * scale * level
    return jnp.minimum(jnp.maximum(drawn, -limit), limit).astype(kind)


def heavy_noise(key, shape, deviation, bound, pieces, heavy, held_as=jnp.bfloat16):
    array = deviation * jax.random.normal(key, shape, jnp.float32)
    if pieces:
        array = array * block_levels(key, shape, pieces, -0.22, 0.18)
    return jnp.clip(with_spikes(array, jax.random.fold_in(key, 3), *heavy), -bound, bound).astype(held_as)


def setup_inputs(seed: int = 0) -> dict:
    arg_keys = jax.random.split(jax.random.key(seed), 8)
    return {
        "queries": draw_queries(jax.random.fold_in(arg_keys[7], 71), 0),
        "keys": draw_keys(jax.random.fold_in(arg_keys[7], 71), 0),
        "values": noise(arg_keys[2], (BATCH, FRAMES, D), 1.0, 6.0, ((0, 2), (1, 8), (2, 2))),
        "out_weight": noise(arg_keys[3], (D, D), D ** -0.5, 0.15625, ((0, 2),)),
        "residual": noise(arg_keys[4], (BATCH, FRAMES, D), 0.2, 1.1953125, ((0, 2), (1, 8), (2, 2))),
        "lengths": jax.random.randint(arg_keys[5], (BATCH,), FRAMES // 2, FRAMES + 1).astype(jnp.int32),
        "grad_out": heavy_noise(arg_keys[6], (BATCH, FRAMES, D), 1.0, 6.0, ((0, 2), (1, 8), (2, 2)), (1, 2, 8, 2.0)),
    }


def reference(queries, keys, values, out_weight, residual, lengths, grad_out):
    scale = 1.0 / math.sqrt(HEAD_DIM)
    span = math.gcd(FRAMES, 512)
    blocks = FRAMES // span
    highest = lax.Precision.HIGHEST
    outputs = []
    grads_q = []
    grads_k = []
    grads_v = []
    grad_weight = jnp.zeros((D, D), jnp.float32)
    for batch in range(BATCH):
        q_all = queries[batch].astype(jnp.float32).reshape(FRAMES, HEADS, HEAD_DIM)
        k_all = keys[batch].astype(jnp.float32).reshape(FRAMES, HEADS, HEAD_DIM)
        v_all = values[batch].astype(jnp.float32).reshape(FRAMES, HEADS, HEAD_DIM)
        valid = jnp.arange(FRAMES, dtype=jnp.int32) < lengths[batch]
        q_blocks = q_all.reshape(blocks, span, HEADS, HEAD_DIM)

        def scores_of(q_block):
            s = jnp.einsum('ihc,jhc->hij', q_block, k_all, precision=highest) * scale
            return jnp.where(valid[None, None, :], s, -1e+30)

        def forward(q_block):
            s = scores_of(q_block)
            top = lax.optimization_barrier(jnp.max(s, axis=2))
            lse = top + jnp.log(lax.optimization_barrier(jnp.sum(jnp.exp(s - top[:, :, None]), axis=2)))
            probs = jnp.exp(s - lse[:, :, None])
            out = jnp.einsum('hij,jhc->ihc', probs, v_all, precision=highest)
            return (out, lse)
        attn_blocks, lse_blocks = lax.map(forward, q_blocks)
        attn_full = attn_blocks.reshape(FRAMES, HEADS, HEAD_DIM)
        attn = attn_full.reshape(FRAMES, D).astype(jnp.bfloat16)
        mixed = jnp.dot(attn, out_weight, preferred_element_type=jnp.float32)
        outputs.append((residual[batch].astype(jnp.float32) + mixed).astype(jnp.bfloat16))
        grad_attn = jnp.dot(grad_out[batch], out_weight.T, preferred_element_type=jnp.float32).astype(jnp.bfloat16)
        grad_weight = grad_weight + jnp.dot(attn.T, grad_out[batch], preferred_element_type=jnp.float32)
        g_all = grad_attn.astype(jnp.float32).reshape(FRAMES, HEADS, HEAD_DIM)
        delta = lax.optimization_barrier(jnp.sum(g_all * attn_full, axis=2))

        def backward(state, inputs):
            grad_k, grad_v = state
            q_block, g_block, lse_block, delta_block = inputs
            s = scores_of(q_block)
            probs = jnp.exp(s - lse_block[:, :, None])
            dots = jnp.einsum('ihc,jhc->hij', g_block, v_all, precision=highest)
            dscores = lax.optimization_barrier((probs * (dots - delta_block.T[:, :, None]) * scale).astype(jnp.bfloat16)).astype(jnp.float32)
            probs_low = lax.optimization_barrier(probs.astype(jnp.bfloat16)).astype(jnp.float32)
            grad_q = jnp.einsum('hij,jhc->ihc', dscores, k_all, precision=highest).astype(jnp.bfloat16)
            grad_k = grad_k + jnp.einsum('hij,ihc->jhc', dscores, q_block, precision=highest)
            grad_v = grad_v + jnp.einsum('hij,ihc->jhc', probs_low, g_block, precision=highest)
            return ((grad_k, grad_v), grad_q)
        empty = jnp.zeros((FRAMES, HEADS, HEAD_DIM), jnp.float32)
        (grad_k, grad_v), grad_q = lax.scan(backward, (empty, empty), (q_blocks, g_all.reshape(blocks, span, HEADS, HEAD_DIM), lse_blocks, delta.reshape(blocks, span, HEADS)))
        grads_q.append(grad_q.reshape(FRAMES, D))
        grads_k.append(grad_k.reshape(FRAMES, D).astype(jnp.bfloat16))
        grads_v.append(grad_v.reshape(FRAMES, D).astype(jnp.bfloat16))
    return (jnp.stack(outputs), jnp.stack(grads_q), jnp.stack(grads_k), jnp.stack(grads_v), grad_weight)
```

```python
import math

import jax
import jax.numpy as jnp
from jax import lax
from jax.sharding import PartitionSpec as P

HEAD_DIM = 96


block_rows = 1024


def split_heads(rows):
    return rows.reshape(rows.shape[0], -1, HEAD_DIM)


def join_heads(blocks):
    return jnp.transpose(blocks, (1, 0, 2)).reshape(blocks.shape[1], -1)


def by_blocks(step_fn, carry, piece):
    count = piece[0].shape[0]
    size = count if count <= block_rows else math.gcd(count, block_rows)

    def one(index, state):
        first = index * size
        part = tuple((lax.dynamic_slice_in_dim(item, first, size, 0) for item in piece))
        return step_fn(state, part, first)

    return lax.fori_loop(0, count // size, one, carry)


def shards(queries, keys, values, out_weight, residual, lengths, grad_out):
    scale = 1.0 / math.sqrt(HEAD_DIM)
    highest = lax.Precision.HIGHEST
    own_q = queries[0]
    own_k = keys[0]
    own_v = values[0]
    frames_here = own_q.shape[0]
    length = lengths[0]
    q_heads = split_heads(own_q)
    k_heads = split_heads(own_k)
    v_heads = split_heads(own_v)
    heads_here = q_heads.shape[1]
    key_pos = lax.axis_index("seq") * frames_here + jnp.arange(frames_here, dtype=jnp.int32)

    def masked_scores(left, right, positions):
        s = jnp.einsum("ihc,jhc->hij", left, right, preferred_element_type=jnp.float32) * scale
        return jnp.where(positions[None, None, :] < length, s, -1e30)

    def forward_step(state, part, start):
        run_max, run_sum, total = state
        k_rows, v_rows = part
        positions = start + jnp.arange(k_rows.shape[0], dtype=jnp.int32)
        s = masked_scores(q_heads, split_heads(k_rows), positions)
        new_max = jnp.maximum(run_max, jnp.max(s, axis=2))
        factor = jnp.exp(run_max - new_max)
        weights = jnp.exp(s - new_max[:, :, None])
        run_sum = run_sum * factor + jnp.sum(weights, axis=2)
        total = total * factor[:, :, None] + jnp.einsum(
            "hij,jhc->hic", weights, split_heads(v_rows).astype(jnp.float32), precision=highest
        )
        return (new_max, run_sum, total)

    start_state = (
        jnp.full((heads_here, frames_here), -1e30, jnp.float32),
        jnp.zeros((heads_here, frames_here), jnp.float32),
        jnp.zeros((heads_here, frames_here, HEAD_DIM), jnp.float32),
    )
    grad_full = lax.all_gather(grad_out[0], "tensor", axis=1, tiled=True)
    grad_attn = lax.dot_general(
        grad_full, out_weight, (((1,), (1,)), ((), ())), preferred_element_type=jnp.float32
    ).astype(jnp.bfloat16)
    width = own_k.shape[1]
    kv_all = lax.all_gather(jnp.concatenate([own_k, own_v], axis=1), "seq", axis=0, tiled=True)
    qg_all = lax.all_gather(jnp.concatenate([own_q, grad_attn], axis=1), "seq", axis=0, tiled=True)
    k_all = kv_all[:, :width]
    v_all = kv_all[:, width:]
    run_max, run_sum, total = by_blocks(forward_step, start_state, (k_all, v_all))
    log_sum = run_max + jnp.log(run_sum)
    attn_full = total / run_sum[:, :, None]
    attn = join_heads(attn_full).astype(jnp.bfloat16)
    partial_out = jnp.dot(attn, out_weight, preferred_element_type=jnp.float32)
    mixed = lax.psum_scatter(
        partial_out.astype(jnp.bfloat16), "tensor", scatter_dimension=1, tiled=True
    ).astype(jnp.float32)
    block_out = (residual[0].astype(jnp.float32) + mixed).astype(jnp.bfloat16)
    weight_term = lax.dot_general(
        attn, grad_full, (((0,), (0,)), ((), ())), preferred_element_type=jnp.float32
    )
    grad_weight = lax.psum_scatter(
        weight_term.astype(jnp.bfloat16), ("dp", "seq"), scatter_dimension=1, tiled=True
    ).astype(jnp.float32)
    g_heads = split_heads(grad_attn)
    delta = jnp.sum(jnp.transpose(g_heads, (1, 0, 2)).astype(jnp.float32) * attn_full, axis=2)

    def query_step(grad_q, part, start):
        k_rows, v_rows = part
        positions = start + jnp.arange(k_rows.shape[0], dtype=jnp.int32)
        s = masked_scores(q_heads, split_heads(k_rows), positions)
        probs = jnp.exp(s - log_sum[:, :, None])
        dots = jnp.einsum(
            "ihc,jhc->hij", g_heads, split_heads(v_rows), preferred_element_type=jnp.float32
        )
        dscores = (probs * (dots - delta[:, :, None]) * scale).astype(jnp.bfloat16)
        return grad_q + jnp.einsum(
            "hij,jhc->hic", dscores, split_heads(k_rows), preferred_element_type=jnp.float32
        )

    empty_q = jnp.zeros((heads_here, frames_here, HEAD_DIM), jnp.float32)
    grad_q = by_blocks(query_step, empty_q, (k_all, v_all))
    stats = lax.all_gather(jnp.concatenate([log_sum, delta], axis=0), "seq", axis=1, tiled=True)

    def key_step(state, part, start):
        grad_k, grad_v = state
        q_rows, g_rows, lse_rows, delta_rows = part
        q_part = split_heads(q_rows.astype(jnp.bfloat16))
        g_part = split_heads(g_rows.astype(jnp.bfloat16))
        s = masked_scores(q_part, k_heads, key_pos)
        probs = jnp.exp(s - lse_rows.T[:, :, None])
        dots = jnp.einsum("ihc,jhc->hij", g_part, v_heads, preferred_element_type=jnp.float32)
        dscores = (probs * (dots - delta_rows.T[:, :, None]) * scale).astype(jnp.bfloat16)
        grad_k = grad_k + jnp.einsum(
            "hij,ihc->hjc", dscores, q_part, preferred_element_type=jnp.float32
        )
        grad_v = grad_v + jnp.einsum(
            "hij,ihc->hjc", probs.astype(jnp.bfloat16), g_part, preferred_element_type=jnp.float32
        )
        return (grad_k, grad_v)

    grad_k, grad_v = by_blocks(
        key_step,
        (empty_q, empty_q),
        (
            qg_all[:, :width],
            qg_all[:, width:],
            stats[:heads_here].T,
            stats[heads_here:].T,
        ),
    )
    return (
        block_out[None],
        join_heads(grad_q).astype(jnp.bfloat16)[None],
        join_heads(grad_k).astype(jnp.bfloat16)[None],
        join_heads(grad_v).astype(jnp.bfloat16)[None],
        grad_weight,
    )


def solution(mesh):
    in_specs = (
        P("dp", "seq", "tensor"),
        P("dp", "seq", "tensor"),
        P("dp", "seq", "tensor"),
        P("tensor", None),
        P("dp", "seq", "tensor"),
        P("dp"),
        P("dp", "seq", "tensor"),
    )
    out_specs = (
        P("dp", "seq", "tensor"),
        P("dp", "seq", "tensor"),
        P("dp", "seq", "tensor"),
        P("dp", "seq", "tensor"),
        P("tensor", ("dp", "seq")),
    )
    return jax.shard_map(shards, mesh=mesh, in_specs=in_specs, out_specs=out_specs, check_vma=False)
```

```python
import math

import jax
import jax.numpy as jnp
from jax import lax
from jax.sharding import PartitionSpec as P

HEAD_DIM = 96


def split_heads(rows):
    return rows.reshape(rows.shape[0], -1, HEAD_DIM)


def join_heads(blocks):
    return jnp.transpose(blocks, (1, 0, 2)).reshape(blocks.shape[1], -1)


def shifted_blocks(x, axis_name, n):
    blocks = [x]
    for k in range(1, n):
        perm = [(i, (i + k) % n) for i in range(n)]
        blocks.append(lax.ppermute(x, axis_name, perm))
    return blocks


def shards(queries, keys, values, out_weight, residual, lengths, grad_out):
    scale = 1.0 / math.sqrt(HEAD_DIM)
    highest = lax.Precision.HIGHEST
    n_seq = lax.axis_size("seq")
    n_dp = lax.axis_size("dp")
    me = lax.axis_index("seq")
    own_q = queries[0]
    own_k = keys[0]
    own_v = values[0]
    frames_here = own_q.shape[0]
    width = own_q.shape[1]
    length = lengths[0]
    q_heads = split_heads(own_q)
    k_heads = split_heads(own_k)
    v_heads = split_heads(own_v)
    heads_here = q_heads.shape[1]
    frame_ids = jnp.arange(frames_here, dtype=jnp.int32)
    key_pos = me * frames_here + frame_ids

    def source_of(k):
        return (me - k + n_seq) % n_seq

    def masked_scores(left, right, positions):
        s = jnp.einsum("ihc,jhc->hij", left, right, preferred_element_type=jnp.float32) * scale
        return jnp.where(positions[None, None, :] < length, s, -1e30)

    grad_full = lax.all_gather(grad_out[0], "tensor", axis=1, tiled=True)
    grad_attn = lax.dot_general(
        grad_full, out_weight, (((1,), (1,)), ((), ())), preferred_element_type=jnp.float32
    ).astype(jnp.bfloat16)
    g_heads = split_heads(grad_attn)

    kv_blocks = shifted_blocks(jnp.concatenate([own_k, own_v], axis=1), "seq", n_seq)
    qg_blocks = shifted_blocks(jnp.concatenate([own_q, grad_attn], axis=1), "seq", n_seq)

    run_max = jnp.full((heads_here, frames_here), -1e30, jnp.float32)
    run_sum = jnp.zeros((heads_here, frames_here), jnp.float32)
    total = jnp.zeros((heads_here, frames_here, HEAD_DIM), jnp.float32)
    for k, kv in enumerate(kv_blocks):
        positions = source_of(k) * frames_here + frame_ids
        s = masked_scores(q_heads, split_heads(kv[:, :width]), positions)
        new_max = jnp.maximum(run_max, jnp.max(s, axis=2))
        factor = jnp.exp(run_max - new_max)
        weights = jnp.exp(s - new_max[:, :, None])
        run_sum = run_sum * factor + jnp.sum(weights, axis=2)
        total = total * factor[:, :, None] + jnp.einsum(
            "hij,jhc->hic", weights, split_heads(kv[:, width:]).astype(jnp.float32), precision=highest
        )
        run_max = new_max
    log_sum = run_max + jnp.log(run_sum)
    attn_full = total / run_sum[:, :, None]
    attn = join_heads(attn_full).astype(jnp.bfloat16)
    partial_out = jnp.dot(attn, out_weight, preferred_element_type=jnp.float32)
    mixed = lax.psum_scatter(
        partial_out.astype(jnp.bfloat16), "tensor", scatter_dimension=1, tiled=True
    ).astype(jnp.float32)
    block_out = (residual[0].astype(jnp.float32) + mixed).astype(jnp.bfloat16)

    delta = jnp.sum(jnp.transpose(g_heads, (1, 0, 2)).astype(jnp.float32) * attn_full, axis=2)
    stat_blocks = shifted_blocks(jnp.concatenate([log_sum, delta], axis=0), "seq", n_seq)

    col_width = grad_full.shape[1] // (n_dp * n_seq)
    g_cols = grad_full.reshape(frames_here, n_dp, n_seq, col_width)
    ag_blocks = []
    for k in range(n_seq):
        target = (me + k) % n_seq
        cols = lax.dynamic_index_in_dim(g_cols, target, axis=2, keepdims=False)
        piece = jnp.concatenate([attn, cols.reshape(frames_here, n_dp * col_width)], axis=1)
        if k == 0:
            ag_blocks.append(piece)
        else:
            perm = [(i, (i + k) % n_seq) for i in range(n_seq)]
            ag_blocks.append(lax.ppermute(piece, "seq", perm))
    weight_term = jnp.zeros((width, n_dp * col_width), jnp.float32)
    for piece in ag_blocks:
        weight_term = weight_term + lax.dot_general(
            piece[:, :width], piece[:, width:], (((0,), (0,)), ((), ())),
            preferred_element_type=jnp.float32,
        )
    grad_weight = lax.psum_scatter(weight_term, "dp", scatter_dimension=1, tiled=True)

    grad_q = jnp.zeros((heads_here, frames_here, HEAD_DIM), jnp.float32)
    for k, kv in enumerate(kv_blocks):
        positions = source_of(k) * frames_here + frame_ids
        k_rows = split_heads(kv[:, :width])
        s = masked_scores(q_heads, k_rows, positions)
        probs = jnp.exp(s - log_sum[:, :, None])
        dots = jnp.einsum(
            "ihc,jhc->hij", g_heads, split_heads(kv[:, width:]), preferred_element_type=jnp.float32
        )
        dscores = (probs * (dots - delta[:, :, None]) * scale).astype(jnp.bfloat16)
        grad_q = grad_q + jnp.einsum("hij,jhc->hic", dscores, k_rows, preferred_element_type=jnp.float32)

    grad_k = jnp.zeros((heads_here, frames_here, HEAD_DIM), jnp.float32)
    grad_v = jnp.zeros((heads_here, frames_here, HEAD_DIM), jnp.float32)
    for qg, stats in zip(qg_blocks, stat_blocks):
        q_part = split_heads(qg[:, :width])
        g_part = split_heads(qg[:, width:])
        s = masked_scores(q_part, k_heads, key_pos)
        probs = jnp.exp(s - stats[:heads_here][:, :, None])
        dots = jnp.einsum("ihc,jhc->hij", g_part, v_heads, preferred_element_type=jnp.float32)
        dscores = (probs * (dots - stats[heads_here:][:, :, None]) * scale).astype(jnp.bfloat16)
        grad_k = grad_k + jnp.einsum("hij,ihc->hjc", dscores, q_part, preferred_element_type=jnp.float32)
        grad_v = grad_v + jnp.einsum(
            "hij,ihc->hjc", probs.astype(jnp.bfloat16), g_part, preferred_element_type=jnp.float32
        )
    return (
        block_out[None],
        join_heads(grad_q).astype(jnp.bfloat16)[None],
        join_heads(grad_k).astype(jnp.bfloat16)[None],
        join_heads(grad_v).astype(jnp.bfloat16)[None],
        grad_weight,
    )


def solution(mesh):
    in_specs = (
        P("dp", "seq", "tensor"),
        P("dp", "seq", "tensor"),
        P("dp", "seq", "tensor"),
        P("tensor", None),
        P("dp", "seq", "tensor"),
        P("dp"),
        P("dp", "seq", "tensor"),
    )
    out_specs = (
        P("dp", "seq", "tensor"),
        P("dp", "seq", "tensor"),
        P("dp", "seq", "tensor"),
        P("dp", "seq", "tensor"),
        P("tensor", ("dp", "seq")),
    )
    return jax.shard_map(shards, mesh=mesh, in_specs=in_specs, out_specs=out_specs, check_vma=False)
```

```python
import math

import jax
import jax.numpy as jnp
from jax import lax
from jax.sharding import PartitionSpec as P

HEAD_DIM = 96


block_rows = 1024


def split_heads(rows):
    return rows.reshape(rows.shape[0], -1, HEAD_DIM)


def join_heads(blocks):
    return jnp.transpose(blocks, (1, 0, 2)).reshape(blocks.shape[1], -1)


def by_blocks(step_fn, carry, piece):
    count = piece[0].shape[0]
    size = count if count <= block_rows else math.gcd(count, block_rows)

    def one(index, state):
        first = index * size
        part = tuple((lax.dynamic_slice_in_dim(item, first, size, 0) for item in piece))
        return step_fn(state, part, first)

    return lax.fori_loop(0, count // size, one, carry)


def shards(queries, keys, values, out_weight, residual, lengths, grad_out):
    scale = 1.0 / math.sqrt(HEAD_DIM)
    highest = lax.Precision.HIGHEST
    own_q = queries[0]
    own_k = keys[0]
    own_v = values[0]
    frames_here = own_q.shape[0]
    length = lengths[0]
    q_heads = split_heads(own_q)
    k_heads = split_heads(own_k)
    v_heads = split_heads(own_v)
    heads_here = q_heads.shape[1]
    key_pos = lax.axis_index("seq") * frames_here + jnp.arange(frames_here, dtype=jnp.int32)

    def masked_scores(left, right, positions):
        s = jnp.einsum("ihc,jhc->hij", left, right, preferred_element_type=jnp.float32) * scale
        return jnp.where(positions[None, None, :] < length, s, -1e30)

    def forward_step(state, part, start):
        run_max, run_sum, total = state
        k_rows, v_rows = part
        positions = start + jnp.arange(k_rows.shape[0], dtype=jnp.int32)
        s = masked_scores(q_heads, split_heads(k_rows), positions)
        new_max = jnp.maximum(run_max, jnp.max(s, axis=2))
        factor = jnp.exp(run_max - new_max)
        weights = jnp.exp(s - new_max[:, :, None])
        run_sum = run_sum * factor + jnp.sum(weights, axis=2)
        total = total * factor[:, :, None] + jnp.einsum(
            "hij,jhc->hic", weights, split_heads(v_rows).astype(jnp.float32), precision=highest
        )
        return (new_max, run_sum, total)

    start_state = (
        jnp.full((heads_here, frames_here), -1e30, jnp.float32),
        jnp.zeros((heads_here, frames_here), jnp.float32),
        jnp.zeros((heads_here, frames_here, HEAD_DIM), jnp.float32),
    )
    grad_full = lax.all_gather(grad_out[0], "tensor", axis=1, tiled=True)
    grad_attn = lax.dot_general(
        grad_full, out_weight, (((1,), (1,)), ((), ())), preferred_element_type=jnp.float32
    ).astype(jnp.bfloat16)
    width = own_k.shape[1]
    kv_all = lax.all_gather(jnp.concatenate([own_k, own_v], axis=1), "seq", axis=0, tiled=True)
    qg_all = lax.all_gather(jnp.concatenate([own_q, grad_attn], axis=1), "seq", axis=0, tiled=True)
    k_all = kv_all[:, :width]
    v_all = kv_all[:, width:]
    run_max, run_sum, total = by_blocks(forward_step, start_state, (k_all, v_all))
    log_sum = run_max + jnp.log(run_sum)
    attn_full = total / run_sum[:, :, None]
    attn = join_heads(attn_full).astype(jnp.bfloat16)
    partial_out = jnp.dot(attn, out_weight, preferred_element_type=jnp.float32)
    mixed = lax.psum_scatter(
        partial_out.astype(jnp.bfloat16), "tensor", scatter_dimension=1, tiled=True
    ).astype(jnp.float32)
    block_out = (residual[0].astype(jnp.float32) + mixed).astype(jnp.bfloat16)
    n_seq = lax.axis_size("seq")
    n_dp = lax.axis_size("dp")
    col_width = grad_full.shape[1] // (n_dp * n_seq)
    g_cols = jnp.transpose(grad_full.reshape(frames_here, n_dp, n_seq, col_width), (0, 2, 1, 3))
    g_mine = lax.all_to_all(
        g_cols.reshape(frames_here, n_seq * n_dp * col_width), "seq", 1, 0, tiled=True
    )
    attn_all = lax.all_gather(attn, "seq", axis=0, tiled=True)
    weight_term = lax.dot_general(
        attn_all, g_mine, (((0,), (0,)), ((), ())), preferred_element_type=jnp.float32
    )
    grad_weight = lax.psum_scatter(weight_term, "dp", scatter_dimension=1, tiled=True)
    g_heads = split_heads(grad_attn)
    delta = jnp.sum(jnp.transpose(g_heads, (1, 0, 2)).astype(jnp.float32) * attn_full, axis=2)

    def query_step(grad_q, part, start):
        k_rows, v_rows = part
        positions = start + jnp.arange(k_rows.shape[0], dtype=jnp.int32)
        s = masked_scores(q_heads, split_heads(k_rows), positions)
        probs = jnp.exp(s - log_sum[:, :, None])
        dots = jnp.einsum(
            "ihc,jhc->hij", g_heads, split_heads(v_rows), preferred_element_type=jnp.float32
        )
        dscores = (probs * (dots - delta[:, :, None]) * scale).astype(jnp.bfloat16)
        return grad_q + jnp.einsum(
            "hij,jhc->hic", dscores, split_heads(k_rows), preferred_element_type=jnp.float32
        )

    empty_q = jnp.zeros((heads_here, frames_here, HEAD_DIM), jnp.float32)
    grad_q = by_blocks(query_step, empty_q, (k_all, v_all))
    stats = lax.psum(
        lax.dynamic_update_slice_in_dim(
            jnp.zeros((2 * heads_here, n_seq * frames_here), jnp.float32),
            jnp.concatenate([log_sum, delta], axis=0),
            lax.axis_index("seq") * frames_here,
            axis=1,
        ),
        "seq",
    )

    def key_step(state, part, start):
        grad_k, grad_v = state
        q_rows, g_rows, lse_rows, delta_rows = part
        q_part = split_heads(q_rows.astype(jnp.bfloat16))
        g_part = split_heads(g_rows.astype(jnp.bfloat16))
        s = masked_scores(q_part, k_heads, key_pos)
        probs = jnp.exp(s - lse_rows.T[:, :, None])
        dots = jnp.einsum("ihc,jhc->hij", g_part, v_heads, preferred_element_type=jnp.float32)
        dscores = (probs * (dots - delta_rows.T[:, :, None]) * scale).astype(jnp.bfloat16)
        grad_k = grad_k + jnp.einsum(
            "hij,ihc->hjc", dscores, q_part, preferred_element_type=jnp.float32
        )
        grad_v = grad_v + jnp.einsum(
            "hij,ihc->hjc", probs.astype(jnp.bfloat16), g_part, preferred_element_type=jnp.float32
        )
        return (grad_k, grad_v)

    grad_k, grad_v = by_blocks(
        key_step,
        (empty_q, empty_q),
        (
            qg_all[:, :width],
            qg_all[:, width:],
            stats[:heads_here].T,
            stats[heads_here:].T,
        ),
    )
    return (
        block_out[None],
        join_heads(grad_q).astype(jnp.bfloat16)[None],
        join_heads(grad_k).astype(jnp.bfloat16)[None],
        join_heads(grad_v).astype(jnp.bfloat16)[None],
        grad_weight,
    )


def solution(mesh):
    in_specs = (
        P("dp", "seq", "tensor"),
        P("dp", "seq", "tensor"),
        P("dp", "seq", "tensor"),
        P("tensor", None),
        P("dp", "seq", "tensor"),
        P("dp"),
        P("dp", "seq", "tensor"),
    )
    out_specs = (
        P("dp", "seq", "tensor"),
        P("dp", "seq", "tensor"),
        P("dp", "seq", "tensor"),
        P("dp", "seq", "tensor"),
        P("tensor", ("dp", "seq")),
    )
    return jax.shard_map(shards, mesh=mesh, in_specs=in_specs, out_specs=out_specs, check_vma=False)
```

```python
import math

import jax
import jax.numpy as jnp
from jax import lax
from jax.sharding import PartitionSpec as P

HEAD_DIM = 96


block_rows = 1024


def split_heads(rows):
    return rows.reshape(rows.shape[0], -1, HEAD_DIM)


def join_heads(blocks):
    return jnp.transpose(blocks, (1, 0, 2)).reshape(blocks.shape[1], -1)


def gather_rows(x, axis_name):
    n = lax.axis_size(axis_name)
    spread = jnp.broadcast_to(x[None], (n,) + x.shape)
    return lax.all_to_all(spread, axis_name, 0, 0, tiled=True)


def scatter_sum(x, axis_name, axis):
    n = lax.axis_size(axis_name)
    shape = x.shape[:axis] + (n, x.shape[axis] // n) + x.shape[axis + 1:]
    pieces = jnp.moveaxis(x.reshape(shape), axis, 0)
    return jnp.sum(lax.all_to_all(pieces, axis_name, 0, 0, tiled=True), axis=0)


def by_blocks(step_fn, carry, piece):
    count = piece[0].shape[0]
    size = count if count <= block_rows else math.gcd(count, block_rows)

    def one(index, state):
        first = index * size
        part = tuple((lax.dynamic_slice_in_dim(item, first, size, 0) for item in piece))
        return step_fn(state, part, first)

    return lax.fori_loop(0, count // size, one, carry)


def shards(queries, keys, values, out_weight, residual, lengths, grad_out):
    scale = 1.0 / math.sqrt(HEAD_DIM)
    highest = lax.Precision.HIGHEST
    own_q = queries[0]
    own_k = keys[0]
    own_v = values[0]
    frames_here = own_q.shape[0]
    length = lengths[0]
    q_heads = split_heads(own_q)
    k_heads = split_heads(own_k)
    v_heads = split_heads(own_v)
    heads_here = q_heads.shape[1]
    key_pos = lax.axis_index("seq") * frames_here + jnp.arange(frames_here, dtype=jnp.int32)

    def masked_scores(left, right, positions):
        s = jnp.einsum("ihc,jhc->hij", left, right, preferred_element_type=jnp.float32) * scale
        return jnp.where(positions[None, None, :] < length, s, -1e30)

    def forward_step(state, part, start):
        run_max, run_sum, total = state
        k_rows, v_rows = part
        positions = start + jnp.arange(k_rows.shape[0], dtype=jnp.int32)
        s = masked_scores(q_heads, split_heads(k_rows), positions)
        new_max = jnp.maximum(run_max, jnp.max(s, axis=2))
        factor = jnp.exp(run_max - new_max)
        weights = jnp.exp(s - new_max[:, :, None])
        run_sum = run_sum * factor + jnp.sum(weights, axis=2)
        total = total * factor[:, :, None] + jnp.einsum(
            "hij,jhc->hic", weights, split_heads(v_rows).astype(jnp.float32), precision=highest
        )
        return (new_max, run_sum, total)

    start_state = (
        jnp.full((heads_here, frames_here), -1e30, jnp.float32),
        jnp.zeros((heads_here, frames_here), jnp.float32),
        jnp.zeros((heads_here, frames_here, HEAD_DIM), jnp.float32),
    )
    grad_full = lax.all_gather(grad_out[0], "tensor", axis=1, tiled=True)
    grad_attn = lax.dot_general(
        grad_full, out_weight, (((1,), (1,)), ((), ())), preferred_element_type=jnp.float32
    ).astype(jnp.bfloat16)
    width = own_k.shape[1]
    kv_all = gather_rows(jnp.concatenate([own_k, own_v], axis=1), "seq").reshape(-1, 2 * own_k.shape[1])
    qg_all = gather_rows(jnp.concatenate([own_q, grad_attn], axis=1), "seq").reshape(-1, 2 * own_k.shape[1])
    k_all = kv_all[:, :width]
    v_all = kv_all[:, width:]
    run_max, run_sum, total = by_blocks(forward_step, start_state, (k_all, v_all))
    log_sum = run_max + jnp.log(run_sum)
    attn_full = total / run_sum[:, :, None]
    attn = join_heads(attn_full).astype(jnp.bfloat16)
    partial_out = jnp.dot(attn, out_weight, preferred_element_type=jnp.float32)
    mixed = scatter_sum(partial_out, "tensor", 1)
    block_out = (residual[0].astype(jnp.float32) + mixed).astype(jnp.bfloat16)
    n_seq = lax.axis_size("seq")
    n_dp = lax.axis_size("dp")
    col_width = grad_full.shape[1] // (n_dp * n_seq)
    g_cols = jnp.transpose(grad_full.reshape(frames_here, n_dp, n_seq, col_width), (0, 2, 1, 3))
    g_mine = lax.all_to_all(
        g_cols.reshape(frames_here, n_seq * n_dp * col_width), "seq", 1, 0, tiled=True
    )
    attn_all = gather_rows(attn, "seq").reshape(-1, attn.shape[1])
    weight_term = lax.dot_general(
        attn_all, g_mine, (((0,), (0,)), ((), ())), preferred_element_type=jnp.float32
    )
    grad_weight = scatter_sum(weight_term, "dp", 1)
    g_heads = split_heads(grad_attn)
    delta = jnp.sum(jnp.transpose(g_heads, (1, 0, 2)).astype(jnp.float32) * attn_full, axis=2)

    def query_step(grad_q, part, start):
        k_rows, v_rows = part
        positions = start + jnp.arange(k_rows.shape[0], dtype=jnp.int32)
        s = masked_scores(q_heads, split_heads(k_rows), positions)
        probs = jnp.exp(s - log_sum[:, :, None])
        dots = jnp.einsum(
            "ihc,jhc->hij", g_heads, split_heads(v_rows), preferred_element_type=jnp.float32
        )
        dscores = (probs * (dots - delta[:, :, None]) * scale).astype(jnp.bfloat16)
        return grad_q + jnp.einsum(
            "hij,jhc->hic", dscores, split_heads(k_rows), preferred_element_type=jnp.float32
        )

    empty_q = jnp.zeros((heads_here, frames_here, HEAD_DIM), jnp.float32)
    grad_q = by_blocks(query_step, empty_q, (k_all, v_all))
    stats = gather_rows(jnp.concatenate([log_sum, delta], axis=0), "seq")
    stats = jnp.transpose(stats, (1, 0, 2)).reshape(2 * heads_here, -1)

    def key_step(state, part, start):
        grad_k, grad_v = state
        q_rows, g_rows, lse_rows, delta_rows = part
        q_part = split_heads(q_rows.astype(jnp.bfloat16))
        g_part = split_heads(g_rows.astype(jnp.bfloat16))
        s = masked_scores(q_part, k_heads, key_pos)
        probs = jnp.exp(s - lse_rows.T[:, :, None])
        dots = jnp.einsum("ihc,jhc->hij", g_part, v_heads, preferred_element_type=jnp.float32)
        dscores = (probs * (dots - delta_rows.T[:, :, None]) * scale).astype(jnp.bfloat16)
        grad_k = grad_k + jnp.einsum(
            "hij,ihc->hjc", dscores, q_part, preferred_element_type=jnp.float32
        )
        grad_v = grad_v + jnp.einsum(
            "hij,ihc->hjc", probs.astype(jnp.bfloat16), g_part, preferred_element_type=jnp.float32
        )
        return (grad_k, grad_v)

    grad_k, grad_v = by_blocks(
        key_step,
        (empty_q, empty_q),
        (
            qg_all[:, :width],
            qg_all[:, width:],
            stats[:heads_here].T,
            stats[heads_here:].T,
        ),
    )
    return (
        block_out[None],
        join_heads(grad_q).astype(jnp.bfloat16)[None],
        join_heads(grad_k).astype(jnp.bfloat16)[None],
        join_heads(grad_v).astype(jnp.bfloat16)[None],
        grad_weight,
    )


def solution(mesh):
    in_specs = (
        P("dp", "seq", "tensor"),
        P("dp", "seq", "tensor"),
        P("dp", "seq", "tensor"),
        P("tensor", None),
        P("dp", "seq", "tensor"),
        P("dp"),
        P("dp", "seq", "tensor"),
    )
    out_specs = (
        P("dp", "seq", "tensor"),
        P("dp", "seq", "tensor"),
        P("dp", "seq", "tensor"),
        P("dp", "seq", "tensor"),
        P("tensor", ("dp", "seq")),
    )
    return jax.shard_map(shards, mesh=mesh, in_specs=in_specs, out_specs=out_specs, check_vma=False)
```

```python
import math

import jax
import jax.numpy as jnp
from jax import lax
from jax.sharding import PartitionSpec as P


HEAD_DIM = 96


block_rows = 1024


def split_heads(rows):
    return rows.reshape(rows.shape[0], -1, HEAD_DIM)


def join_heads(blocks):
    return jnp.transpose(blocks, (1, 0, 2)).reshape(blocks.shape[1], -1)


def gather_rows(x, axis_name):
    n = lax.axis_size(axis_name)
    spread = jnp.broadcast_to(x[None], (n,) + x.shape)
    return lax.all_to_all(spread, axis_name, 0, 0, tiled=True)


def scatter_sum(x, axis_name, axis):
    n = lax.axis_size(axis_name)
    shape = x.shape[:axis] + (n, x.shape[axis] // n) + x.shape[axis + 1:]
    pieces = jnp.moveaxis(x.reshape(shape), axis, 0)
    return jnp.sum(lax.all_to_all(pieces, axis_name, 0, 0, tiled=True), axis=0)


def by_blocks(step_fn, carry, piece):
    count = piece[0].shape[0]
    size = count if count <= block_rows else math.gcd(count, block_rows)

    def one(index, state):
        first = index * size
        part = tuple((lax.dynamic_slice_in_dim(item, first, size, 0) for item in piece))
        return step_fn(state, part, first)

    return lax.fori_loop(0, count // size, one, carry)


def shards_body(queries, keys, values, out_weight, residual, lengths, grad_out):
    scale = 1.0 / math.sqrt(HEAD_DIM)
    highest = lax.Precision.HIGHEST
    own_q = queries[0]
    own_k = keys[0]
    own_v = values[0]
    frames_here = own_q.shape[0]
    length = lengths[0]
    q_heads = split_heads(own_q)
    k_heads = split_heads(own_k)
    v_heads = split_heads(own_v)
    heads_here = q_heads.shape[1]
    key_pos = lax.axis_index("seq") * frames_here + jnp.arange(frames_here, dtype=jnp.int32)

    def masked_scores(left, right, positions):
        s = jnp.einsum("ihc,jhc->hij", left, right, preferred_element_type=jnp.float32) * scale
        return jnp.where(positions[None, None, :] < length, s, -1e30)

    def forward_step(state, part, start):
        run_max, run_sum, total = state
        k_rows, v_rows = part
        positions = start + jnp.arange(k_rows.shape[0], dtype=jnp.int32)
        s = masked_scores(q_heads, split_heads(k_rows), positions)
        new_max = jnp.maximum(run_max, jnp.max(s, axis=2))
        factor = jnp.exp(run_max - new_max)
        weights = jnp.exp(s - new_max[:, :, None])
        run_sum = run_sum * factor + jnp.sum(weights, axis=2)
        total = total * factor[:, :, None] + jnp.einsum(
            "hij,jhc->hic", weights, split_heads(v_rows).astype(jnp.float32), precision=highest
        )
        return (new_max, run_sum, total)

    start_state = (
        jnp.full((heads_here, frames_here), -1e30, jnp.float32),
        jnp.zeros((heads_here, frames_here), jnp.float32),
        jnp.zeros((heads_here, frames_here, HEAD_DIM), jnp.float32),
    )
    grad_full = lax.all_gather(grad_out[0], "tensor", axis=1, tiled=True)
    grad_attn = lax.dot_general(
        grad_full, out_weight, (((1,), (1,)), ((), ())), preferred_element_type=jnp.float32
    ).astype(jnp.bfloat16)
    width = own_k.shape[1]
    kv_rows = jnp.concatenate([own_k, own_v], axis=1)
    kv_all = lax.all_gather(kv_rows, "seq", axis=0, tiled=True)
    n_seq = lax.axis_size("seq")
    n_dp = lax.axis_size("dp")
    col_width = grad_full.shape[1] // (n_dp * n_seq)
    g_cols = jnp.transpose(grad_full.reshape(frames_here, n_dp, n_seq, col_width), (2, 0, 1, 3))
    g_cols = g_cols.reshape(n_seq, frames_here, n_dp * col_width)
    qg_spread = jnp.broadcast_to(
        jnp.concatenate([own_q, grad_attn], axis=1)[None], (n_seq, frames_here, 2 * width)
    )
    outgoing = jnp.concatenate([qg_spread, g_cols], axis=2)
    moved = lax.all_to_all(outgoing, "seq", 0, 0, tiled=True)
    qg_all = moved[:, :, : 2 * width].reshape(-1, 2 * width)
    g_mine = moved[:, :, 2 * width :].reshape(-1, n_dp * col_width)
    k_all = kv_all[:, :width]
    v_all = kv_all[:, width:]
    run_max, run_sum, total = by_blocks(forward_step, start_state, (k_all, v_all))
    log_sum = run_max + jnp.log(run_sum)
    attn_full = total / run_sum[:, :, None]
    attn = join_heads(attn_full).astype(jnp.bfloat16)
    partial_out = jnp.dot(attn, out_weight, preferred_element_type=jnp.float32)
    mixed = scatter_sum(partial_out, "tensor", 1)
    block_out = (residual[0].astype(jnp.float32) + mixed).astype(jnp.bfloat16)
    attn_all = lax.all_gather(attn, "seq", axis=0, tiled=True)
    weight_term = lax.dot_general(
        attn_all, g_mine, (((0,), (0,)), ((), ())), preferred_element_type=jnp.float32
    )
    grad_weight = scatter_sum(weight_term, "dp", 1)
    g_heads = split_heads(grad_attn)
    delta = jnp.sum(jnp.transpose(g_heads, (1, 0, 2)).astype(jnp.float32) * attn_full, axis=2)

    def query_step(grad_q, part, start):
        k_rows, v_rows = part
        positions = start + jnp.arange(k_rows.shape[0], dtype=jnp.int32)
        s = masked_scores(q_heads, split_heads(k_rows), positions)
        probs = jnp.exp(s - log_sum[:, :, None])
        dots = jnp.einsum(
            "ihc,jhc->hij", g_heads, split_heads(v_rows), preferred_element_type=jnp.float32
        )
        dscores = (probs * (dots - delta[:, :, None]) * scale).astype(jnp.bfloat16)
        return grad_q + jnp.einsum(
            "hij,jhc->hic", dscores, split_heads(k_rows), preferred_element_type=jnp.float32
        )

    empty_q = jnp.zeros((heads_here, frames_here, HEAD_DIM), jnp.float32)
    grad_q = by_blocks(query_step, empty_q, (k_all, v_all))
    stats = gather_rows(jnp.concatenate([log_sum, delta], axis=0), "seq")
    stats = jnp.transpose(stats, (1, 0, 2)).reshape(2 * heads_here, -1)

    def key_step(state, part, start):
        grad_k, grad_v = state
        q_rows, g_rows, lse_rows, delta_rows = part
        q_part = split_heads(q_rows.astype(jnp.bfloat16))
        g_part = split_heads(g_rows.astype(jnp.bfloat16))
        s = masked_scores(q_part, k_heads, key_pos)
        probs = jnp.exp(s - lse_rows.T[:, :, None])
        dots = jnp.einsum("ihc,jhc->hij", g_part, v_heads, preferred_element_type=jnp.float32)
        dscores = (probs * (dots - delta_rows.T[:, :, None]) * scale).astype(jnp.bfloat16)
        grad_k = grad_k + jnp.einsum(
            "hij,ihc->hjc", dscores, q_part, preferred_element_type=jnp.float32
        )
        grad_v = grad_v + jnp.einsum(
            "hij,ihc->hjc", probs.astype(jnp.bfloat16), g_part, preferred_element_type=jnp.float32
        )
        return (grad_k, grad_v)

    grad_k, grad_v = by_blocks(
        key_step,
        (empty_q, empty_q),
        (
            qg_all[:, :width],
            qg_all[:, width:],
            stats[:heads_here].T,
            stats[heads_here:].T,
        ),
    )
    return (
        block_out[None],
        join_heads(grad_q).astype(jnp.bfloat16)[None],
        join_heads(grad_k).astype(jnp.bfloat16)[None],
        join_heads(grad_v).astype(jnp.bfloat16)[None],
        grad_weight,
    )


def solution(mesh):
    in_specs = (
        P("dp", "seq", "tensor"),
        P("dp", "seq", "tensor"),
        P("dp", "seq", "tensor"),
        P("tensor", None),
        P("dp", "seq", "tensor"),
        P("dp"),
        P("dp", "seq", "tensor"),
    )
    out_specs = (
        P("dp", "seq", "tensor"),
        P("dp", "seq", "tensor"),
        P("dp", "seq", "tensor"),
        P("dp", "seq", "tensor"),
        P("tensor", ("dp", "seq")),
    )
    return jax.shard_map(shards_body, mesh=mesh, in_specs=in_specs, out_specs=out_specs, check_vma=False)
```

```python
import math

import jax
import jax.numpy as jnp
from jax import lax
from jax.sharding import PartitionSpec as P


HEAD_DIM = 96


block_rows = 1024


def split_heads(rows):
    return rows.reshape(rows.shape[0], -1, HEAD_DIM)


def join_heads(blocks):
    return jnp.transpose(blocks, (1, 0, 2)).reshape(blocks.shape[1], -1)


def gather_rows(x, axis_name):
    n = lax.axis_size(axis_name)
    spread = jnp.broadcast_to(x[None], (n,) + x.shape)
    return lax.all_to_all(spread, axis_name, 0, 0, tiled=True)


def ring_gather(x, axis_name, flat=False):
    n = lax.axis_size(axis_name)
    me = lax.axis_index(axis_name)
    if n % 2 == 0:
        ring = list(range(0, n, 2)) + list(range(n - 1, 0, -2))
    else:
        ring = list(range(n))
    place = [0] * n
    for i, d in enumerate(ring):
        place[d] = i
    ring_ids = jnp.array(ring, jnp.int32)
    here = jnp.array(place, jnp.int32)[me]
    to_next = [(ring[i], ring[(i + 1) % n]) for i in range(n)]
    to_prev = [(ring[(i + 1) % n], ring[i]) for i in range(n)]
    if flat:
        gathered = jnp.zeros((n * x.shape[0],) + x.shape[1:], x.dtype)

        def put(buffer, block, source):
            return lax.dynamic_update_slice_in_dim(buffer, block, source * x.shape[0], 0)
    else:
        gathered = jnp.zeros((n,) + x.shape, x.dtype)

        def put(buffer, block, source):
            return lax.dynamic_update_index_in_dim(buffer, block, source, 0)
    gathered = put(gathered, x, me)
    ahead = x
    behind = x
    for step in range(1, n // 2 + 1):
        ahead = lax.ppermute(ahead, axis_name, to_next)
        source = ring_ids[(here - step + n) % n]
        gathered = put(gathered, ahead, source)
        if step <= (n - 1) // 2:
            behind = lax.ppermute(behind, axis_name, to_prev)
            source = ring_ids[(here + step) % n]
            gathered = put(gathered, behind, source)
    return gathered


def scatter_sum(x, axis_name, axis):
    n = lax.axis_size(axis_name)
    shape = x.shape[:axis] + (n, x.shape[axis] // n) + x.shape[axis + 1:]
    pieces = jnp.moveaxis(x.reshape(shape), axis, 0)
    return jnp.sum(lax.all_to_all(pieces, axis_name, 0, 0, tiled=True), axis=0)


def by_blocks(step_fn, carry, piece):
    count = piece[0].shape[0]
    size = count if count <= block_rows else math.gcd(count, block_rows)

    def one(index, state):
        first = index * size
        part = tuple((lax.dynamic_slice_in_dim(item, first, size, 0) for item in piece))
        return step_fn(state, part, first)

    return lax.fori_loop(0, count // size, one, carry)


def shards_body(queries, keys, values, out_weight, residual, lengths, grad_out):
    scale = 1.0 / math.sqrt(HEAD_DIM)
    highest = lax.Precision.HIGHEST
    own_q = queries[0]
    own_k = keys[0]
    own_v = values[0]
    frames_here = own_q.shape[0]
    length = lengths[0]
    q_heads = split_heads(own_q)
    k_heads = split_heads(own_k)
    v_heads = split_heads(own_v)
    heads_here = q_heads.shape[1]
    key_pos = lax.axis_index("seq") * frames_here + jnp.arange(frames_here, dtype=jnp.int32)

    def masked_scores(left, right, positions):
        s = jnp.einsum("ihc,jhc->hij", left, right, preferred_element_type=jnp.float32) * scale
        return jnp.where(positions[None, None, :] < length, s, -1e30)

    def forward_step(state, part, start):
        run_max, run_sum, total = state
        k_rows, v_rows = part
        positions = start + jnp.arange(k_rows.shape[0], dtype=jnp.int32)
        s = masked_scores(q_heads, split_heads(k_rows), positions)
        new_max = jnp.maximum(run_max, jnp.max(s, axis=2))
        factor = jnp.exp(run_max - new_max)
        weights = jnp.exp(s - new_max[:, :, None])
        run_sum = run_sum * factor + jnp.sum(weights, axis=2)
        total = total * factor[:, :, None] + jnp.einsum(
            "hij,jhc->hic", weights, split_heads(v_rows).astype(jnp.float32), precision=highest
        )
        return (new_max, run_sum, total)

    start_state = (
        jnp.full((heads_here, frames_here), -1e30, jnp.float32),
        jnp.zeros((heads_here, frames_here), jnp.float32),
        jnp.zeros((heads_here, frames_here, HEAD_DIM), jnp.float32),
    )
    grad_full = lax.all_gather(grad_out[0], "tensor", axis=1, tiled=True)
    grad_attn = lax.dot_general(
        grad_full, out_weight, (((1,), (1,)), ((), ())), preferred_element_type=jnp.float32
    ).astype(jnp.bfloat16)
    width = own_k.shape[1]
    kv_rows = jnp.concatenate([own_k, own_v], axis=1)
    kv_all = ring_gather(kv_rows, "seq").reshape(-1, 2 * width)
    n_seq = lax.axis_size("seq")
    n_dp = lax.axis_size("dp")
    col_width = grad_full.shape[1] // (n_dp * n_seq)
    g_cols = jnp.transpose(grad_full.reshape(frames_here, n_dp, n_seq, col_width), (2, 0, 1, 3))
    g_cols = g_cols.reshape(n_seq, frames_here, n_dp * col_width)
    g_mine = lax.all_to_all(g_cols, "seq", 0, 0, tiled=True).reshape(-1, n_dp * col_width)
    qg_rows = jnp.concatenate([own_q, grad_attn], axis=1)
    qg_all = ring_gather(qg_rows, "seq", flat=True)
    k_all = kv_all[:, :width]
    v_all = kv_all[:, width:]
    run_max, run_sum, total = by_blocks(forward_step, start_state, (k_all, v_all))
    log_sum = run_max + jnp.log(run_sum)
    attn_full = total / run_sum[:, :, None]
    attn = join_heads(attn_full).astype(jnp.bfloat16)
    partial_out = jnp.dot(attn, out_weight, preferred_element_type=jnp.float32)
    mixed = scatter_sum(partial_out, "tensor", 1)
    block_out = (residual[0].astype(jnp.float32) + mixed).astype(jnp.bfloat16)
    attn_all = lax.all_gather(attn, "seq", axis=0, tiled=True)
    weight_term = lax.dot_general(
        attn_all, g_mine, (((0,), (0,)), ((), ())), preferred_element_type=jnp.float32
    )
    grad_weight = scatter_sum(weight_term, "dp", 1)
    g_heads = split_heads(grad_attn)
    delta = jnp.sum(jnp.transpose(g_heads, (1, 0, 2)).astype(jnp.float32) * attn_full, axis=2)

    def query_step(grad_q, part, start):
        k_rows, v_rows = part
        positions = start + jnp.arange(k_rows.shape[0], dtype=jnp.int32)
        s = masked_scores(q_heads, split_heads(k_rows), positions)
        probs = jnp.exp(s - log_sum[:, :, None])
        dots = jnp.einsum(
            "ihc,jhc->hij", g_heads, split_heads(v_rows), preferred_element_type=jnp.float32
        )
        dscores = (probs * (dots - delta[:, :, None]) * scale).astype(jnp.bfloat16)
        return grad_q + jnp.einsum(
            "hij,jhc->hic", dscores, split_heads(k_rows), preferred_element_type=jnp.float32
        )

    empty_q = jnp.zeros((heads_here, frames_here, HEAD_DIM), jnp.float32)
    grad_q = by_blocks(query_step, empty_q, (k_all, v_all))
    stats = gather_rows(jnp.concatenate([log_sum, delta], axis=0), "seq")
    stats = jnp.transpose(stats, (1, 0, 2)).reshape(2 * heads_here, -1)

    def key_step(state, part, start):
        grad_k, grad_v = state
        q_rows, g_rows, lse_rows, delta_rows = part
        q_part = split_heads(q_rows.astype(jnp.bfloat16))
        g_part = split_heads(g_rows.astype(jnp.bfloat16))
        s = masked_scores(q_part, k_heads, key_pos)
        probs = jnp.exp(s - lse_rows.T[:, :, None])
        dots = jnp.einsum("ihc,jhc->hij", g_part, v_heads, preferred_element_type=jnp.float32)
        dscores = (probs * (dots - delta_rows.T[:, :, None]) * scale).astype(jnp.bfloat16)
        grad_k = grad_k + jnp.einsum(
            "hij,ihc->hjc", dscores, q_part, preferred_element_type=jnp.float32
        )
        grad_v = grad_v + jnp.einsum(
            "hij,ihc->hjc", probs.astype(jnp.bfloat16), g_part, preferred_element_type=jnp.float32
        )
        return (grad_k, grad_v)

    grad_k, grad_v = by_blocks(
        key_step,
        (empty_q, empty_q),
        (
            qg_all[:, :width],
            qg_all[:, width:],
            stats[:heads_here].T,
            stats[heads_here:].T,
        ),
    )
    return (
        block_out[None],
        join_heads(grad_q).astype(jnp.bfloat16)[None],
        join_heads(grad_k).astype(jnp.bfloat16)[None],
        join_heads(grad_v).astype(jnp.bfloat16)[None],
        grad_weight,
    )


def solution(mesh):
    in_specs = (
        P("dp", "seq", "tensor"),
        P("dp", "seq", "tensor"),
        P("dp", "seq", "tensor"),
        P("tensor", None),
        P("dp", "seq", "tensor"),
        P("dp"),
        P("dp", "seq", "tensor"),
    )
    out_specs = (
        P("dp", "seq", "tensor"),
        P("dp", "seq", "tensor"),
        P("dp", "seq", "tensor"),
        P("dp", "seq", "tensor"),
        P("tensor", ("dp", "seq")),
    )
    return jax.shard_map(shards_body, mesh=mesh, in_specs=in_specs, out_specs=out_specs, check_vma=False)
```

```python
import math

import jax
import jax.numpy as jnp
from jax import lax
from jax.sharding import PartitionSpec as P


HEAD_DIM = 96


block_rows = 1024


def split_heads(rows):
    return rows.reshape(rows.shape[0], -1, HEAD_DIM)


def join_heads(blocks):
    return jnp.transpose(blocks, (1, 0, 2)).reshape(blocks.shape[1], -1)


def gather_rows(x, axis_name):
    n = lax.axis_size(axis_name)
    spread = jnp.broadcast_to(x[None], (n,) + x.shape)
    return lax.all_to_all(spread, axis_name, 0, 0, tiled=True)


def ring_gather(x, axis_name):
    n = lax.axis_size(axis_name)
    me = lax.axis_index(axis_name)
    if n % 2 == 0:
        ring = list(range(0, n, 2)) + list(range(n - 1, 0, -2))
    else:
        ring = list(range(n))
    place = [0] * n
    for i, d in enumerate(ring):
        place[d] = i
    ring_ids = jnp.array(ring, jnp.int32)
    here = jnp.array(place, jnp.int32)[me]
    to_next = [(ring[i], ring[(i + 1) % n]) for i in range(n)]
    to_prev = [(ring[(i + 1) % n], ring[i]) for i in range(n)]
    gathered = jnp.zeros((n,) + x.shape, x.dtype)
    gathered = lax.dynamic_update_index_in_dim(gathered, x, me, 0)
    ahead = x
    behind = x
    for step in range(1, n // 2 + 1):
        ahead = lax.ppermute(ahead, axis_name, to_next)
        source = ring_ids[(here - step + n) % n]
        gathered = lax.dynamic_update_index_in_dim(gathered, ahead, source, 0)
        if step <= (n - 1) // 2:
            behind = lax.ppermute(behind, axis_name, to_prev)
            source = ring_ids[(here + step) % n]
            gathered = lax.dynamic_update_index_in_dim(gathered, behind, source, 0)
    return gathered


def scatter_sum(x, axis_name, axis):
    n = lax.axis_size(axis_name)
    shape = x.shape[:axis] + (n, x.shape[axis] // n) + x.shape[axis + 1:]
    pieces = jnp.moveaxis(x.reshape(shape), axis, 0)
    return jnp.sum(lax.all_to_all(pieces, axis_name, 0, 0, tiled=True), axis=0)


def by_blocks(step_fn, carry, piece):
    count = piece[0].shape[0]
    size = count if count <= block_rows else math.gcd(count, block_rows)

    def one(index, state):
        first = index * size
        part = tuple((lax.dynamic_slice_in_dim(item, first, size, 0) for item in piece))
        return step_fn(state, part, first)

    return lax.fori_loop(0, count // size, one, carry)


def shards_body(queries, keys, values, out_weight, residual, lengths, grad_out):
    scale = 1.0 / math.sqrt(HEAD_DIM)
    highest = lax.Precision.HIGHEST
    own_q = queries[0]
    own_k = keys[0]
    own_v = values[0]
    frames_here = own_q.shape[0]
    length = lengths[0]
    q_heads = split_heads(own_q)
    k_heads = split_heads(own_k)
    v_heads = split_heads(own_v)
    heads_here = q_heads.shape[1]
    key_pos = lax.axis_index("seq") * frames_here + jnp.arange(frames_here, dtype=jnp.int32)

    def masked_scores(left, right, positions):
        s = jnp.einsum("ihc,jhc->hij", left, right, preferred_element_type=jnp.float32) * scale
        return jnp.where(positions[None, None, :] < length, s, -1e30)

    def forward_step(state, part, start):
        run_max, run_sum, total = state
        k_rows, v_rows = part
        positions = start + jnp.arange(k_rows.shape[0], dtype=jnp.int32)
        s = masked_scores(q_heads, split_heads(k_rows), positions)
        new_max = jnp.maximum(run_max, jnp.max(s, axis=2))
        factor = jnp.exp(run_max - new_max)
        weights = jnp.exp(s - new_max[:, :, None])
        run_sum = run_sum * factor + jnp.sum(weights, axis=2)
        total = total * factor[:, :, None] + jnp.einsum(
            "hij,jhc->hic", weights, split_heads(v_rows).astype(jnp.float32), precision=highest
        )
        return (new_max, run_sum, total)

    start_state = (
        jnp.full((heads_here, frames_here), -1e30, jnp.float32),
        jnp.zeros((heads_here, frames_here), jnp.float32),
        jnp.zeros((heads_here, frames_here, HEAD_DIM), jnp.float32),
    )
    grad_full = lax.all_gather(grad_out[0], "tensor", axis=1, tiled=True)
    grad_attn = lax.dot_general(
        grad_full, out_weight, (((1,), (1,)), ((), ())), preferred_element_type=jnp.float32
    ).astype(jnp.bfloat16)
    width = own_k.shape[1]
    kv_rows = jnp.concatenate([own_k, own_v], axis=1)
    kv_all = ring_gather(kv_rows, "seq").reshape(-1, 2 * width)
    n_seq = lax.axis_size("seq")
    n_dp = lax.axis_size("dp")
    col_width = grad_full.shape[1] // (n_dp * n_seq)
    g_cols = jnp.transpose(grad_full.reshape(frames_here, n_dp, n_seq, col_width), (2, 0, 1, 3))
    g_cols = g_cols.reshape(n_seq, frames_here, n_dp * col_width)
    g_mine = lax.all_to_all(g_cols, "seq", 0, 0, tiled=True).reshape(-1, n_dp * col_width)
    qg_rows = jnp.concatenate([own_q, grad_attn], axis=1)
    qg_all = lax.all_gather(qg_rows, "seq", axis=0, tiled=True)
    k_all = kv_all[:, :width]
    v_all = kv_all[:, width:]
    run_max, run_sum, total = by_blocks(forward_step, start_state, (k_all, v_all))
    log_sum = run_max + jnp.log(run_sum)
    attn_full = total / run_sum[:, :, None]
    attn = join_heads(attn_full).astype(jnp.bfloat16)
    partial_out = jnp.dot(attn, out_weight, preferred_element_type=jnp.float32)
    mixed = scatter_sum(partial_out, "tensor", 1)
    block_out = (residual[0].astype(jnp.float32) + mixed).astype(jnp.bfloat16)
    attn_all = lax.all_gather(attn, "seq", axis=0, tiled=True)
    weight_term = lax.dot_general(
        attn_all, g_mine, (((0,), (0,)), ((), ())), preferred_element_type=jnp.float32
    )
    grad_weight = scatter_sum(weight_term, "dp", 1)
    g_heads = split_heads(grad_attn)
    delta = jnp.sum(jnp.transpose(g_heads, (1, 0, 2)).astype(jnp.float32) * attn_full, axis=2)

    def query_step(grad_q, part, start):
        k_rows, v_rows = part
        positions = start + jnp.arange(k_rows.shape[0], dtype=jnp.int32)
        s = masked_scores(q_heads, split_heads(k_rows), positions)
        probs = jnp.exp(s - log_sum[:, :, None])
        dots = jnp.einsum(
            "ihc,jhc->hij", g_heads, split_heads(v_rows), preferred_element_type=jnp.float32
        )
        dscores = (probs * (dots - delta[:, :, None]) * scale).astype(jnp.bfloat16)
        return grad_q + jnp.einsum(
            "hij,jhc->hic", dscores, split_heads(k_rows), preferred_element_type=jnp.float32
        )

    empty_q = jnp.zeros((heads_here, frames_here, HEAD_DIM), jnp.float32)
    grad_q = by_blocks(query_step, empty_q, (k_all, v_all))
    stats = gather_rows(jnp.concatenate([log_sum, delta], axis=0), "seq")
    stats = jnp.transpose(stats, (1, 0, 2)).reshape(2 * heads_here, -1)

    def key_step(state, part, start):
        grad_k, grad_v = state
        q_rows, g_rows, lse_rows, delta_rows = part
        q_part = split_heads(q_rows.astype(jnp.bfloat16))
        g_part = split_heads(g_rows.astype(jnp.bfloat16))
        s = masked_scores(q_part, k_heads, key_pos)
        probs = jnp.exp(s - lse_rows.T[:, :, None])
        dots = jnp.einsum("ihc,jhc->hij", g_part, v_heads, preferred_element_type=jnp.float32)
        dscores = (probs * (dots - delta_rows.T[:, :, None]) * scale).astype(jnp.bfloat16)
        grad_k = grad_k + jnp.einsum(
            "hij,ihc->hjc", dscores, q_part, preferred_element_type=jnp.float32
        )
        grad_v = grad_v + jnp.einsum(
            "hij,ihc->hjc", probs.astype(jnp.bfloat16), g_part, preferred_element_type=jnp.float32
        )
        return (grad_k, grad_v)

    grad_k, grad_v = by_blocks(
        key_step,
        (empty_q, empty_q),
        (
            qg_all[:, :width],
            qg_all[:, width:],
            stats[:heads_here].T,
            stats[heads_here:].T,
        ),
    )
    return (
        block_out[None],
        join_heads(grad_q).astype(jnp.bfloat16)[None],
        join_heads(grad_k).astype(jnp.bfloat16)[None],
        join_heads(grad_v).astype(jnp.bfloat16)[None],
        grad_weight,
    )


def solution(mesh):
    in_specs = (
        P("dp", "seq", "tensor"),
        P("dp", "seq", "tensor"),
        P("dp", "seq", "tensor"),
        P("tensor", None),
        P("dp", "seq", "tensor"),
        P("dp"),
        P("dp", "seq", "tensor"),
    )
    out_specs = (
        P("dp", "seq", "tensor"),
        P("dp", "seq", "tensor"),
        P("dp", "seq", "tensor"),
        P("dp", "seq", "tensor"),
        P("tensor", ("dp", "seq")),
    )
    return jax.shard_map(shards_body, mesh=mesh, in_specs=in_specs, out_specs=out_specs, check_vma=False)
```

```python
import math

import jax
import jax.numpy as jnp
from jax import lax
from jax.sharding import PartitionSpec as P


HEAD_DIM = 96


block_rows = 1024


def split_heads(rows):
    return rows.reshape(rows.shape[0], -1, HEAD_DIM)


def join_heads(blocks):
    return jnp.transpose(blocks, (1, 0, 2)).reshape(blocks.shape[1], -1)


def gather_rows(x, axis_name):
    n = lax.axis_size(axis_name)
    spread = jnp.broadcast_to(x[None], (n,) + x.shape)
    return lax.all_to_all(spread, axis_name, 0, 0, tiled=True)


def ring_gather(x, axis_name):
    n = lax.axis_size(axis_name)
    me = lax.axis_index(axis_name)
    if n % 2 == 0:
        ring = list(range(0, n, 2)) + list(range(n - 1, 0, -2))
    else:
        ring = list(range(n))
    place = [0] * n
    for i, d in enumerate(ring):
        place[d] = i
    ring_ids = jnp.array(ring, jnp.int32)
    here = jnp.array(place, jnp.int32)[me]
    to_next = [(ring[i], ring[(i + 1) % n]) for i in range(n)]
    to_prev = [(ring[(i + 1) % n], ring[i]) for i in range(n)]
    gathered = jnp.zeros((n,) + x.shape, x.dtype)
    gathered = lax.dynamic_update_index_in_dim(gathered, x, me, 0)
    ahead = x
    behind = x
    for step in range(1, n // 2 + 1):
        ahead = lax.ppermute(ahead, axis_name, to_next)
        source = ring_ids[(here - step + n) % n]
        gathered = lax.dynamic_update_index_in_dim(gathered, ahead, source, 0)
        if step <= (n - 1) // 2:
            behind = lax.ppermute(behind, axis_name, to_prev)
            source = ring_ids[(here + step) % n]
            gathered = lax.dynamic_update_index_in_dim(gathered, behind, source, 0)
    return gathered


def scatter_sum(x, axis_name, axis):
    n = lax.axis_size(axis_name)
    shape = x.shape[:axis] + (n, x.shape[axis] // n) + x.shape[axis + 1:]
    pieces = jnp.moveaxis(x.reshape(shape), axis, 0)
    return jnp.sum(lax.all_to_all(pieces, axis_name, 0, 0, tiled=True), axis=0)


def by_blocks(step_fn, carry, piece):
    count = piece[0].shape[0]
    size = count if count <= block_rows else math.gcd(count, block_rows)

    def one(index, state):
        first = index * size
        part = tuple((lax.dynamic_slice_in_dim(item, first, size, 0) for item in piece))
        return step_fn(state, part, first)

    return lax.fori_loop(0, count // size, one, carry)


def shards_body(queries, keys, values, out_weight, residual, lengths, grad_out):
    scale = 1.0 / math.sqrt(HEAD_DIM)
    highest = lax.Precision.HIGHEST
    own_q = queries[0]
    own_k = keys[0]
    own_v = values[0]
    frames_here = own_q.shape[0]
    length = lengths[0]
    q_heads = split_heads(own_q)
    k_heads = split_heads(own_k)
    v_heads = split_heads(own_v)
    heads_here = q_heads.shape[1]
    key_pos = lax.axis_index("seq") * frames_here + jnp.arange(frames_here, dtype=jnp.int32)

    def masked_scores(left, right, positions):
        s = jnp.einsum("ihc,jhc->hij", left, right, preferred_element_type=jnp.float32) * scale
        return jnp.where(positions[None, None, :] < length, s, -1e30)

    def forward_step(state, part, start):
        run_max, run_sum, total = state
        k_rows, v_rows = part
        positions = start + jnp.arange(k_rows.shape[0], dtype=jnp.int32)
        s = masked_scores(q_heads, split_heads(k_rows), positions)
        new_max = jnp.maximum(run_max, jnp.max(s, axis=2))
        factor = jnp.exp(run_max - new_max)
        weights = jnp.exp(s - new_max[:, :, None])
        run_sum = run_sum * factor + jnp.sum(weights, axis=2)
        total = total * factor[:, :, None] + jnp.einsum(
            "hij,jhc->hic", weights, split_heads(v_rows).astype(jnp.float32), precision=highest
        )
        return (new_max, run_sum, total)

    start_state = (
        jnp.full((heads_here, frames_here), -1e30, jnp.float32),
        jnp.zeros((heads_here, frames_here), jnp.float32),
        jnp.zeros((heads_here, frames_here, HEAD_DIM), jnp.float32),
    )
    grad_full = lax.all_gather(grad_out[0], "tensor", axis=1, tiled=True)
    grad_attn = lax.dot_general(
        grad_full, out_weight, (((1,), (1,)), ((), ())), preferred_element_type=jnp.float32
    ).astype(jnp.bfloat16)
    width = own_k.shape[1]
    kv_rows = jnp.concatenate([own_k, own_v], axis=1)
    kv_all = ring_gather(kv_rows, "seq").reshape(-1, 2 * width)
    n_seq = lax.axis_size("seq")
    n_dp = lax.axis_size("dp")
    col_width = grad_full.shape[1] // (n_dp * n_seq)
    g_cols = jnp.transpose(grad_full.reshape(frames_here, n_dp, n_seq, col_width), (2, 0, 1, 3))
    g_cols = g_cols.reshape(n_seq, frames_here, n_dp * col_width)
    g_mine = lax.all_to_all(g_cols, "seq", 0, 0, tiled=True).reshape(-1, n_dp * col_width)
    qg_all = ring_gather(jnp.concatenate([own_q, grad_attn], axis=1), "seq").reshape(-1, 2 * width)
    k_all = kv_all[:, :width]
    v_all = kv_all[:, width:]
    run_max, run_sum, total = by_blocks(forward_step, start_state, (k_all, v_all))
    log_sum = run_max + jnp.log(run_sum)
    attn_full = total / run_sum[:, :, None]
    attn = join_heads(attn_full).astype(jnp.bfloat16)
    partial_out = jnp.dot(attn, out_weight, preferred_element_type=jnp.float32)
    mixed = lax.psum_scatter(partial_out, "tensor", scatter_dimension=1, tiled=True)
    block_out = (residual[0].astype(jnp.float32) + mixed).astype(jnp.bfloat16)
    attn_all = ring_gather(attn, "seq").reshape(-1, attn.shape[1])
    weight_term = lax.dot_general(
        attn_all, g_mine, (((0,), (0,)), ((), ())), preferred_element_type=jnp.float32
    )
    grad_weight = scatter_sum(weight_term, "dp", 1)
    g_heads = split_heads(grad_attn)
    delta = jnp.sum(jnp.transpose(g_heads, (1, 0, 2)).astype(jnp.float32) * attn_full, axis=2)

    def query_step(grad_q, part, start):
        k_rows, v_rows = part
        positions = start + jnp.arange(k_rows.shape[0], dtype=jnp.int32)
        s = masked_scores(q_heads, split_heads(k_rows), positions)
        probs = jnp.exp(s - log_sum[:, :, None])
        dots = jnp.einsum(
            "ihc,jhc->hij", g_heads, split_heads(v_rows), preferred_element_type=jnp.float32
        )
        dscores = (probs * (dots - delta[:, :, None]) * scale).astype(jnp.bfloat16)
        return grad_q + jnp.einsum(
            "hij,jhc->hic", dscores, split_heads(k_rows), preferred_element_type=jnp.float32
        )

    empty_q = jnp.zeros((heads_here, frames_here, HEAD_DIM), jnp.float32)
    grad_q = by_blocks(query_step, empty_q, (k_all, v_all))
    stats = gather_rows(jnp.concatenate([log_sum, delta], axis=0), "seq")
    stats = jnp.transpose(stats, (1, 0, 2)).reshape(2 * heads_here, -1)

    def key_step(state, part, start):
        grad_k, grad_v = state
        q_rows, g_rows, lse_rows, delta_rows = part
        q_part = split_heads(q_rows.astype(jnp.bfloat16))
        g_part = split_heads(g_rows.astype(jnp.bfloat16))
        s = masked_scores(q_part, k_heads, key_pos)
        probs = jnp.exp(s - lse_rows.T[:, :, None])
        dots = jnp.einsum("ihc,jhc->hij", g_part, v_heads, preferred_element_type=jnp.float32)
        dscores = (probs * (dots - delta_rows.T[:, :, None]) * scale).astype(jnp.bfloat16)
        grad_k = grad_k + jnp.einsum(
            "hij,ihc->hjc", dscores, q_part, preferred_element_type=jnp.float32
        )
        grad_v = grad_v + jnp.einsum(
            "hij,ihc->hjc", probs.astype(jnp.bfloat16), g_part, preferred_element_type=jnp.float32
        )
        return (grad_k, grad_v)

    grad_k, grad_v = by_blocks(
        key_step,
        (empty_q, empty_q),
        (
            qg_all[:, :width],
            qg_all[:, width:],
            stats[:heads_here].T,
            stats[heads_here:].T,
        ),
    )
    return (
        block_out[None],
        join_heads(grad_q).astype(jnp.bfloat16)[None],
        join_heads(grad_k).astype(jnp.bfloat16)[None],
        join_heads(grad_v).astype(jnp.bfloat16)[None],
        grad_weight,
    )


def solution(mesh):
    in_specs = (
        P("dp", "seq", "tensor"),
        P("dp", "seq", "tensor"),
        P("dp", "seq", "tensor"),
        P("tensor", None),
        P("dp", "seq", "tensor"),
        P("dp"),
        P("dp", "seq", "tensor"),
    )
    out_specs = (
        P("dp", "seq", "tensor"),
        P("dp", "seq", "tensor"),
        P("dp", "seq", "tensor"),
        P("dp", "seq", "tensor"),
        P("tensor", ("dp", "seq")),
    )
    return jax.shard_map(shards_body, mesh=mesh, in_specs=in_specs, out_specs=out_specs, check_vma=False)
```

```python
import math

import jax
import jax.numpy as jnp
from jax import lax
from jax.sharding import PartitionSpec as P


HEAD_DIM = 96


block_rows = 1024


def split_heads(rows):
    return rows.reshape(rows.shape[0], -1, HEAD_DIM)


def join_heads(blocks):
    return jnp.transpose(blocks, (1, 0, 2)).reshape(blocks.shape[1], -1)


def gather_rows(x, axis_name):
    n = lax.axis_size(axis_name)
    spread = jnp.broadcast_to(x[None], (n,) + x.shape)
    return lax.all_to_all(spread, axis_name, 0, 0, tiled=True)


def ring_gather(x, axis_name, lead=()):
    n = lax.axis_size(axis_name)
    me = lax.axis_index(axis_name)
    if n % 2 == 0:
        ring = list(range(0, n, 2)) + list(range(n - 1, 0, -2))
    else:
        ring = list(range(n))
    place = [0] * n
    for i, d in enumerate(ring):
        place[d] = i
    ring_ids = jnp.array(ring, jnp.int32)
    here = jnp.array(place, jnp.int32)[me]
    to_next = [(ring[i], ring[(i + 1) % n]) for i in range(n)]
    to_prev = [(ring[(i + 1) % n], ring[i]) for i in range(n)]
    x = x.reshape(lead + x.shape)
    gathered = jnp.zeros((n,) + x.shape, x.dtype)
    gathered = lax.dynamic_update_index_in_dim(gathered, x, me, 0)
    ahead = x
    behind = x
    for step in range(1, n // 2 + 1):
        ahead = lax.ppermute(ahead, axis_name, to_next)
        source = ring_ids[(here - step + n) % n]
        gathered = lax.dynamic_update_index_in_dim(gathered, ahead, source, 0)
        if step <= (n - 1) // 2:
            behind = lax.ppermute(behind, axis_name, to_prev)
            source = ring_ids[(here + step) % n]
            gathered = lax.dynamic_update_index_in_dim(gathered, behind, source, 0)
    return gathered


def scatter_sum(x, axis_name, axis):
    n = lax.axis_size(axis_name)
    shape = x.shape[:axis] + (n, x.shape[axis] // n) + x.shape[axis + 1:]
    pieces = jnp.moveaxis(x.reshape(shape), axis, 0)
    return jnp.sum(lax.all_to_all(pieces, axis_name, 0, 0, tiled=True), axis=0)


def by_blocks(step_fn, carry, piece):
    count = piece[0].shape[0]
    size = count if count <= block_rows else math.gcd(count, block_rows)

    def one(index, state):
        first = index * size
        part = tuple((lax.dynamic_slice_in_dim(item, first, size, 0) for item in piece))
        return step_fn(state, part, first)

    return lax.fori_loop(0, count // size, one, carry)


def shards_body(queries, keys, values, out_weight, residual, lengths, grad_out):
    scale = 1.0 / math.sqrt(HEAD_DIM)
    highest = lax.Precision.HIGHEST
    own_q = queries[0]
    own_k = keys[0]
    own_v = values[0]
    frames_here = own_q.shape[0]
    length = lengths[0]
    q_heads = split_heads(own_q)
    k_heads = split_heads(own_k)
    v_heads = split_heads(own_v)
    heads_here = q_heads.shape[1]
    key_pos = lax.axis_index("seq") * frames_here + jnp.arange(frames_here, dtype=jnp.int32)

    def masked_scores(left, right, positions):
        s = jnp.einsum("ihc,jhc->hij", left, right, preferred_element_type=jnp.float32) * scale
        return jnp.where(positions[None, None, :] < length, s, -1e30)

    def forward_step(state, part, start):
        run_max, run_sum, total = state
        k_rows, v_rows = part
        positions = start + jnp.arange(k_rows.shape[0], dtype=jnp.int32)
        s = masked_scores(q_heads, split_heads(k_rows), positions)
        new_max = jnp.maximum(run_max, jnp.max(s, axis=2))
        factor = jnp.exp(run_max - new_max)
        weights = jnp.exp(s - new_max[:, :, None])
        run_sum = run_sum * factor + jnp.sum(weights, axis=2)
        total = total * factor[:, :, None] + jnp.einsum(
            "hij,jhc->hic", weights, split_heads(v_rows).astype(jnp.float32), precision=highest
        )
        return (new_max, run_sum, total)

    start_state = (
        jnp.full((heads_here, frames_here), -1e30, jnp.float32),
        jnp.zeros((heads_here, frames_here), jnp.float32),
        jnp.zeros((heads_here, frames_here, HEAD_DIM), jnp.float32),
    )
    grad_full = lax.all_gather(grad_out[0], "tensor", axis=1, tiled=True)
    grad_attn = lax.dot_general(
        grad_full, out_weight, (((1,), (1,)), ((), ())), preferred_element_type=jnp.float32
    ).astype(jnp.bfloat16)
    width = own_k.shape[1]
    kv_rows = jnp.concatenate([own_k, own_v], axis=1)
    kv_all = ring_gather(kv_rows, "seq").reshape(-1, 2 * width)
    n_seq = lax.axis_size("seq")
    n_dp = lax.axis_size("dp")
    col_width = grad_full.shape[1] // (n_dp * n_seq)
    g_cols = jnp.transpose(grad_full.reshape(frames_here, n_dp, n_seq, col_width), (2, 0, 1, 3))
    g_cols = g_cols.reshape(n_seq, frames_here, n_dp * col_width)
    g_mine = lax.all_to_all(g_cols, "seq", 0, 0, tiled=True).reshape(-1, n_dp * col_width)
    qg_rows = jnp.concatenate([own_q, grad_attn], axis=1)
    qg_all = ring_gather(qg_rows, "seq", lead=(1,)).reshape(-1, 2 * width)
    k_all = kv_all[:, :width]
    v_all = kv_all[:, width:]
    run_max, run_sum, total = by_blocks(forward_step, start_state, (k_all, v_all))
    log_sum = run_max + jnp.log(run_sum)
    attn_full = total / run_sum[:, :, None]
    attn = join_heads(attn_full).astype(jnp.bfloat16)
    partial_out = jnp.dot(attn, out_weight, preferred_element_type=jnp.float32)
    mixed = lax.psum_scatter(partial_out, "tensor", scatter_dimension=1, tiled=True)
    block_out = (residual[0].astype(jnp.float32) + mixed).astype(jnp.bfloat16)
    attn_all = lax.all_gather(attn, "seq", axis=0, tiled=True)
    weight_term = lax.dot_general(
        attn_all, g_mine, (((0,), (0,)), ((), ())), preferred_element_type=jnp.float32
    )
    grad_weight = scatter_sum(weight_term, "dp", 1)
    g_heads = split_heads(grad_attn)
    delta = jnp.sum(jnp.transpose(g_heads, (1, 0, 2)).astype(jnp.float32) * attn_full, axis=2)

    def query_step(grad_q, part, start):
        k_rows, v_rows = part
        positions = start + jnp.arange(k_rows.shape[0], dtype=jnp.int32)
        s = masked_scores(q_heads, split_heads(k_rows), positions)
        probs = jnp.exp(s - log_sum[:, :, None])
        dots = jnp.einsum(
            "ihc,jhc->hij", g_heads, split_heads(v_rows), preferred_element_type=jnp.float32
        )
        dscores = (probs * (dots - delta[:, :, None]) * scale).astype(jnp.bfloat16)
        return grad_q + jnp.einsum(
            "hij,jhc->hic", dscores, split_heads(k_rows), preferred_element_type=jnp.float32
        )

    empty_q = jnp.zeros((heads_here, frames_here, HEAD_DIM), jnp.float32)
    grad_q = by_blocks(query_step, empty_q, (k_all, v_all))
    stats = gather_rows(jnp.concatenate([log_sum, delta], axis=0), "seq")
    stats = jnp.transpose(stats, (1, 0, 2)).reshape(2 * heads_here, -1)

    def key_step(state, part, start):
        grad_k, grad_v = state
        q_rows, g_rows, lse_rows, delta_rows = part
        q_part = split_heads(q_rows.astype(jnp.bfloat16))
        g_part = split_heads(g_rows.astype(jnp.bfloat16))
        s = masked_scores(q_part, k_heads, key_pos)
        probs = jnp.exp(s - lse_rows.T[:, :, None])
        dots = jnp.einsum("ihc,jhc->hij", g_part, v_heads, preferred_element_type=jnp.float32)
        dscores = (probs * (dots - delta_rows.T[:, :, None]) * scale).astype(jnp.bfloat16)
        grad_k = grad_k + jnp.einsum(
            "hij,ihc->hjc", dscores, q_part, preferred_element_type=jnp.float32
        )
        grad_v = grad_v + jnp.einsum(
            "hij,ihc->hjc", probs.astype(jnp.bfloat16), g_part, preferred_element_type=jnp.float32
        )
        return (grad_k, grad_v)

    grad_k, grad_v = by_blocks(
        key_step,
        (empty_q, empty_q),
        (
            qg_all[:, :width],
            qg_all[:, width:],
            stats[:heads_here].T,
            stats[heads_here:].T,
        ),
    )
    return (
        block_out[None],
        join_heads(grad_q).astype(jnp.bfloat16)[None],
        join_heads(grad_k).astype(jnp.bfloat16)[None],
        join_heads(grad_v).astype(jnp.bfloat16)[None],
        grad_weight,
    )


def solution(mesh):
    in_specs = (
        P("dp", "seq", "tensor"),
        P("dp", "seq", "tensor"),
        P("dp", "seq", "tensor"),
        P("tensor", None),
        P("dp", "seq", "tensor"),
        P("dp"),
        P("dp", "seq", "tensor"),
    )
    out_specs = (
        P("dp", "seq", "tensor"),
        P("dp", "seq", "tensor"),
        P("dp", "seq", "tensor"),
        P("dp", "seq", "tensor"),
        P("tensor", ("dp", "seq")),
    )
    return jax.shard_map(shards_body, mesh=mesh, in_specs=in_specs, out_specs=out_specs, check_vma=False)
```

```python
import math

import jax
import jax.numpy as jnp
from jax import lax
from jax.sharding import PartitionSpec as P


HEAD_DIM = 96


block_rows = 1024


def split_heads(rows):
    return rows.reshape(rows.shape[0], -1, HEAD_DIM)


def join_heads(blocks):
    return jnp.transpose(blocks, (1, 0, 2)).reshape(blocks.shape[1], -1)


def gather_rows(x, axis_name):
    n = lax.axis_size(axis_name)
    spread = jnp.broadcast_to(x[None], (n,) + x.shape)
    return lax.all_to_all(spread, axis_name, 0, 0, tiled=True)


def ring_gather(x, axis_name):
    n = lax.axis_size(axis_name)
    me = lax.axis_index(axis_name)
    if n % 2 == 0:
        ring = list(range(0, n, 2)) + list(range(n - 1, 0, -2))
    else:
        ring = list(range(n))
    place = [0] * n
    for i, d in enumerate(ring):
        place[d] = i
    ring_ids = jnp.array(ring, jnp.int32)
    here = jnp.array(place, jnp.int32)[me]
    to_next = [(ring[i], ring[(i + 1) % n]) for i in range(n)]
    to_prev = [(ring[(i + 1) % n], ring[i]) for i in range(n)]
    gathered = jnp.zeros((n,) + x.shape, x.dtype)
    gathered = lax.dynamic_update_index_in_dim(gathered, x, me, 0)
    ahead = x
    behind = x
    for step in range(1, n // 2 + 1):
        ahead = lax.ppermute(ahead, axis_name, to_next)
        source = ring_ids[(here - step + n) % n]
        gathered = lax.dynamic_update_index_in_dim(gathered, ahead, source, 0)
        if step <= (n - 1) // 2:
            behind = lax.ppermute(behind, axis_name, to_prev)
            source = ring_ids[(here + step) % n]
            gathered = lax.dynamic_update_index_in_dim(gathered, behind, source, 0)
    return gathered


def scatter_sum(x, axis_name, axis):
    n = lax.axis_size(axis_name)
    shape = x.shape[:axis] + (n, x.shape[axis] // n) + x.shape[axis + 1:]
    pieces = jnp.moveaxis(x.reshape(shape), axis, 0)
    return jnp.sum(lax.all_to_all(pieces, axis_name, 0, 0, tiled=True), axis=0)


def by_blocks(step_fn, carry, piece):
    count = piece[0].shape[0]
    size = count if count <= block_rows else math.gcd(count, block_rows)

    def one(index, state):
        first = index * size
        part = tuple((lax.dynamic_slice_in_dim(item, first, size, 0) for item in piece))
        return step_fn(state, part, first)

    return lax.fori_loop(0, count // size, one, carry)


def shards_body(queries, keys, values, out_weight, residual, lengths, grad_out):
    scale = 1.0 / math.sqrt(HEAD_DIM)
    highest = lax.Precision.HIGHEST
    own_q = queries[0]
    own_k = keys[0]
    own_v = values[0]
    frames_here = own_q.shape[0]
    length = lengths[0]
    q_heads = split_heads(own_q)
    k_heads = split_heads(own_k)
    v_heads = split_heads(own_v)
    heads_here = q_heads.shape[1]
    key_pos = lax.axis_index("seq") * frames_here + jnp.arange(frames_here, dtype=jnp.int32)

    def masked_scores(left, right, positions):
        s = jnp.einsum("ihc,jhc->hij", left, right, preferred_element_type=jnp.float32) * scale
        return jnp.where(positions[None, None, :] < length, s, -1e30)

    def forward_step(state, part, start):
        run_max, run_sum, total = state
        k_rows, v_rows = part
        positions = start + jnp.arange(k_rows.shape[0], dtype=jnp.int32)
        s = masked_scores(q_heads, split_heads(k_rows), positions)
        new_max = jnp.maximum(run_max, jnp.max(s, axis=2))
        factor = jnp.exp(run_max - new_max)
        weights = jnp.exp(s - new_max[:, :, None])
        run_sum = run_sum * factor + jnp.sum(weights, axis=2)
        total = total * factor[:, :, None] + jnp.einsum(
            "hij,jhc->hic", weights, split_heads(v_rows).astype(jnp.float32), precision=highest
        )
        return (new_max, run_sum, total)

    start_state = (
        jnp.full((heads_here, frames_here), -1e30, jnp.float32),
        jnp.zeros((heads_here, frames_here), jnp.float32),
        jnp.zeros((heads_here, frames_here, HEAD_DIM), jnp.float32),
    )
    grad_full = lax.all_gather(grad_out[0], "tensor", axis=1, tiled=True)
    grad_attn = lax.dot_general(
        grad_full, out_weight, (((1,), (1,)), ((), ())), preferred_element_type=jnp.float32
    ).astype(jnp.bfloat16)
    width = own_k.shape[1]
    kv_rows = jnp.concatenate([own_k, own_v], axis=1)
    everything = ring_gather(
        jnp.concatenate([kv_rows, own_q, grad_attn], axis=1), "seq"
    ).reshape(-1, 4 * width)
    kv_all = everything[:, : 2 * width]
    qg_all = everything[:, 2 * width :]
    n_seq = lax.axis_size("seq")
    n_dp = lax.axis_size("dp")
    col_width = grad_full.shape[1] // (n_dp * n_seq)
    g_cols = jnp.transpose(grad_full.reshape(frames_here, n_dp, n_seq, col_width), (2, 0, 1, 3))
    g_cols = g_cols.reshape(n_seq, frames_here, n_dp * col_width)
    g_mine = lax.all_to_all(g_cols, "seq", 0, 0, tiled=True).reshape(-1, n_dp * col_width)
    k_all = kv_all[:, :width]
    v_all = kv_all[:, width:]
    run_max, run_sum, total = by_blocks(forward_step, start_state, (k_all, v_all))
    log_sum = run_max + jnp.log(run_sum)
    attn_full = total / run_sum[:, :, None]
    attn = join_heads(attn_full).astype(jnp.bfloat16)
    partial_out = jnp.dot(attn, out_weight, preferred_element_type=jnp.float32)
    mixed = scatter_sum(partial_out, "tensor", 1)
    block_out = (residual[0].astype(jnp.float32) + mixed).astype(jnp.bfloat16)
    attn_all = lax.all_gather(attn, "seq", axis=0, tiled=True)
    weight_term = lax.dot_general(
        attn_all, g_mine, (((0,), (0,)), ((), ())), preferred_element_type=jnp.float32
    )
    grad_weight = scatter_sum(weight_term, "dp", 1)
    g_heads = split_heads(grad_attn)
    delta = jnp.sum(jnp.transpose(g_heads, (1, 0, 2)).astype(jnp.float32) * attn_full, axis=2)

    def query_step(grad_q, part, start):
        k_rows, v_rows = part
        positions = start + jnp.arange(k_rows.shape[0], dtype=jnp.int32)
        s = masked_scores(q_heads, split_heads(k_rows), positions)
        probs = jnp.exp(s - log_sum[:, :, None])
        dots = jnp.einsum(
            "ihc,jhc->hij", g_heads, split_heads(v_rows), preferred_element_type=jnp.float32
        )
        dscores = (probs * (dots - delta[:, :, None]) * scale).astype(jnp.bfloat16)
        return grad_q + jnp.einsum(
            "hij,jhc->hic", dscores, split_heads(k_rows), preferred_element_type=jnp.float32
        )

    empty_q = jnp.zeros((heads_here, frames_here, HEAD_DIM), jnp.float32)
    grad_q = by_blocks(query_step, empty_q, (k_all, v_all))
    stats = gather_rows(jnp.concatenate([log_sum, delta], axis=0), "seq")
    stats = jnp.transpose(stats, (1, 0, 2)).reshape(2 * heads_here, -1)

    def key_step(state, part, start):
        grad_k, grad_v = state
        q_rows, g_rows, lse_rows, delta_rows = part
        q_part = split_heads(q_rows.astype(jnp.bfloat16))
        g_part = split_heads(g_rows.astype(jnp.bfloat16))
        s = masked_scores(q_part, k_heads, key_pos)
        probs = jnp.exp(s - lse_rows.T[:, :, None])
        dots = jnp.einsum("ihc,jhc->hij", g_part, v_heads, preferred_element_type=jnp.float32)
        dscores = (probs * (dots - delta_rows.T[:, :, None]) * scale).astype(jnp.bfloat16)
        grad_k = grad_k + jnp.einsum(
            "hij,ihc->hjc", dscores, q_part, preferred_element_type=jnp.float32
        )
        grad_v = grad_v + jnp.einsum(
            "hij,ihc->hjc", probs.astype(jnp.bfloat16), g_part, preferred_element_type=jnp.float32
        )
        return (grad_k, grad_v)

    grad_k, grad_v = by_blocks(
        key_step,
        (empty_q, empty_q),
        (
            qg_all[:, :width],
            qg_all[:, width:],
            stats[:heads_here].T,
            stats[heads_here:].T,
        ),
    )
    return (
        block_out[None],
        join_heads(grad_q).astype(jnp.bfloat16)[None],
        join_heads(grad_k).astype(jnp.bfloat16)[None],
        join_heads(grad_v).astype(jnp.bfloat16)[None],
        grad_weight,
    )


def solution(mesh):
    in_specs = (
        P("dp", "seq", "tensor"),
        P("dp", "seq", "tensor"),
        P("dp", "seq", "tensor"),
        P("tensor", None),
        P("dp", "seq", "tensor"),
        P("dp"),
        P("dp", "seq", "tensor"),
    )
    out_specs = (
        P("dp", "seq", "tensor"),
        P("dp", "seq", "tensor"),
        P("dp", "seq", "tensor"),
        P("dp", "seq", "tensor"),
        P("tensor", ("dp", "seq")),
    )
    return jax.shard_map(shards_body, mesh=mesh, in_specs=in_specs, out_specs=out_specs, check_vma=False)
```

```python
import math

import jax
import jax.numpy as jnp
from jax import lax
from jax.sharding import PartitionSpec as P


HEAD_DIM = 96


block_rows = 1024


def split_heads(rows):
    return rows.reshape(rows.shape[0], -1, HEAD_DIM)


def join_heads(blocks):
    return jnp.transpose(blocks, (1, 0, 2)).reshape(blocks.shape[1], -1)


def gather_rows(x, axis_name):
    n = lax.axis_size(axis_name)
    spread = jnp.broadcast_to(x[None], (n,) + x.shape)
    return lax.all_to_all(spread, axis_name, 0, 0, tiled=True)


def ring_gather(x, axis_name):
    n = lax.axis_size(axis_name)
    me = lax.axis_index(axis_name)
    if n % 2 == 0:
        ring = list(range(0, n, 2)) + list(range(n - 1, 0, -2))
    else:
        ring = list(range(n))
    place = [0] * n
    for i, d in enumerate(ring):
        place[d] = i
    ring_ids = jnp.array(ring, jnp.int32)
    here = jnp.array(place, jnp.int32)[me]
    to_next = [(ring[i], ring[(i + 1) % n]) for i in range(n)]
    to_prev = [(ring[(i + 1) % n], ring[i]) for i in range(n)]
    gathered = jnp.zeros((n,) + x.shape, x.dtype)
    gathered = lax.dynamic_update_index_in_dim(gathered, x, me, 0)
    ahead = x
    behind = x
    for step in range(1, n // 2 + 1):
        ahead = lax.ppermute(ahead, axis_name, to_next)
        source = ring_ids[(here - step + n) % n]
        gathered = lax.dynamic_update_index_in_dim(gathered, ahead, source, 0)
        if step <= (n - 1) // 2:
            behind = lax.ppermute(behind, axis_name, to_prev)
            source = ring_ids[(here + step) % n]
            gathered = lax.dynamic_update_index_in_dim(gathered, behind, source, 0)
    return gathered


def scatter_sum(x, axis_name, axis):
    n = lax.axis_size(axis_name)
    shape = x.shape[:axis] + (n, x.shape[axis] // n) + x.shape[axis + 1:]
    pieces = jnp.moveaxis(x.reshape(shape), axis, 0)
    return jnp.sum(lax.all_to_all(pieces, axis_name, 0, 0, tiled=True), axis=0)


def by_blocks(step_fn, carry, piece):
    count = piece[0].shape[0]
    size = count if count <= block_rows else math.gcd(count, block_rows)

    def one(index, state):
        first = index * size
        part = tuple((lax.dynamic_slice_in_dim(item, first, size, 0) for item in piece))
        return step_fn(state, part, first)

    return lax.fori_loop(0, count // size, one, carry)


def shards_body(queries, keys, values, out_weight, residual, lengths, grad_out):
    scale = 1.0 / math.sqrt(HEAD_DIM)
    highest = lax.Precision.HIGH
    own_q = queries[0]
    own_k = keys[0]
    own_v = values[0]
    frames_here = own_q.shape[0]
    length = lengths[0]
    q_heads = split_heads(own_q)
    k_heads = split_heads(own_k)
    v_heads = split_heads(own_v)
    heads_here = q_heads.shape[1]
    key_pos = lax.axis_index("seq") * frames_here + jnp.arange(frames_here, dtype=jnp.int32)

    def masked_scores(left, right, positions):
        s = jnp.einsum("ihc,jhc->hij", left, right, preferred_element_type=jnp.float32) * scale
        return jnp.where(positions[None, None, :] < length, s, -1e30)

    def forward_step(state, part, start):
        run_max, run_sum, total = state
        k_rows, v_rows = part
        positions = start + jnp.arange(k_rows.shape[0], dtype=jnp.int32)
        s = masked_scores(q_heads, split_heads(k_rows), positions)
        new_max = jnp.maximum(run_max, jnp.max(s, axis=2))
        factor = jnp.exp(run_max - new_max)
        weights = jnp.exp(s - new_max[:, :, None])
        run_sum = run_sum * factor + jnp.sum(weights, axis=2)
        total = total * factor[:, :, None] + jnp.einsum(
            "hij,jhc->hic", weights, split_heads(v_rows).astype(jnp.float32), precision=highest
        )
        return (new_max, run_sum, total)

    start_state = (
        jnp.full((heads_here, frames_here), -1e30, jnp.float32),
        jnp.zeros((heads_here, frames_here), jnp.float32),
        jnp.zeros((heads_here, frames_here, HEAD_DIM), jnp.float32),
    )
    grad_full = lax.all_gather(grad_out[0], "tensor", axis=1, tiled=True)
    grad_attn = lax.dot_general(
        grad_full, out_weight, (((1,), (1,)), ((), ())), preferred_element_type=jnp.float32
    ).astype(jnp.bfloat16)
    width = own_k.shape[1]
    kv_rows = jnp.concatenate([own_k, own_v], axis=1)
    kv_all = ring_gather(kv_rows, "seq").reshape(-1, 2 * width)
    n_seq = lax.axis_size("seq")
    n_dp = lax.axis_size("dp")
    col_width = grad_full.shape[1] // (n_dp * n_seq)
    g_cols = jnp.transpose(grad_full.reshape(frames_here, n_dp, n_seq, col_width), (2, 0, 1, 3))
    g_cols = g_cols.reshape(n_seq, frames_here, n_dp * col_width)
    g_mine = lax.all_to_all(g_cols, "seq", 0, 0, tiled=True).reshape(-1, n_dp * col_width)
    qg_all = ring_gather(jnp.concatenate([own_q, grad_attn], axis=1), "seq").reshape(-1, 2 * width)
    k_all = kv_all[:, :width]
    v_all = kv_all[:, width:]
    run_max, run_sum, total = by_blocks(forward_step, start_state, (k_all, v_all))
    log_sum = run_max + jnp.log(run_sum)
    attn_full = total / run_sum[:, :, None]
    attn = join_heads(attn_full).astype(jnp.bfloat16)
    partial_out = jnp.dot(attn, out_weight, preferred_element_type=jnp.float32)
    mixed = scatter_sum(partial_out, "tensor", 1)
    block_out = (residual[0].astype(jnp.float32) + mixed).astype(jnp.bfloat16)
    attn_all = lax.all_gather(attn, "seq", axis=0, tiled=True)
    weight_term = lax.dot_general(
        attn_all, g_mine, (((0,), (0,)), ((), ())), preferred_element_type=jnp.float32
    )
    grad_weight = scatter_sum(weight_term, "dp", 1)
    g_heads = split_heads(grad_attn)
    delta = jnp.sum(jnp.transpose(g_heads, (1, 0, 2)).astype(jnp.float32) * attn_full, axis=2)

    def query_step(grad_q, part, start):
        k_rows, v_rows = part
        positions = start + jnp.arange(k_rows.shape[0], dtype=jnp.int32)
        s = masked_scores(q_heads, split_heads(k_rows), positions)
        probs = jnp.exp(s - log_sum[:, :, None])
        dots = jnp.einsum(
            "ihc,jhc->hij", g_heads, split_heads(v_rows), preferred_element_type=jnp.float32
        )
        dscores = (probs * (dots - delta[:, :, None]) * scale).astype(jnp.bfloat16)
        return grad_q + jnp.einsum(
            "hij,jhc->hic", dscores, split_heads(k_rows), preferred_element_type=jnp.float32
        )

    empty_q = jnp.zeros((heads_here, frames_here, HEAD_DIM), jnp.float32)
    grad_q = by_blocks(query_step, empty_q, (k_all, v_all))
    stats = gather_rows(jnp.concatenate([log_sum, delta], axis=0), "seq")
    stats = jnp.transpose(stats, (1, 0, 2)).reshape(2 * heads_here, -1)

    def key_step(state, part, start):
        grad_k, grad_v = state
        q_rows, g_rows, lse_rows, delta_rows = part
        q_part = split_heads(q_rows.astype(jnp.bfloat16))
        g_part = split_heads(g_rows.astype(jnp.bfloat16))
        s = masked_scores(q_part, k_heads, key_pos)
        probs = jnp.exp(s - lse_rows.T[:, :, None])
        dots = jnp.einsum("ihc,jhc->hij", g_part, v_heads, preferred_element_type=jnp.float32)
        dscores = (probs * (dots - delta_rows.T[:, :, None]) * scale).astype(jnp.bfloat16)
        grad_k = grad_k + jnp.einsum(
            "hij,ihc->hjc", dscores, q_part, preferred_element_type=jnp.float32
        )
        grad_v = grad_v + jnp.einsum(
            "hij,ihc->hjc", probs.astype(jnp.bfloat16), g_part, preferred_element_type=jnp.float32
        )
        return (grad_k, grad_v)

    grad_k, grad_v = by_blocks(
        key_step,
        (empty_q, empty_q),
        (
            qg_all[:, :width],
            qg_all[:, width:],
            stats[:heads_here].T,
            stats[heads_here:].T,
        ),
    )
    return (
        block_out[None],
        join_heads(grad_q).astype(jnp.bfloat16)[None],
        join_heads(grad_k).astype(jnp.bfloat16)[None],
        join_heads(grad_v).astype(jnp.bfloat16)[None],
        grad_weight,
    )


def solution(mesh):
    in_specs = (
        P("dp", "seq", "tensor"),
        P("dp", "seq", "tensor"),
        P("dp", "seq", "tensor"),
        P("tensor", None),
        P("dp", "seq", "tensor"),
        P("dp"),
        P("dp", "seq", "tensor"),
    )
    out_specs = (
        P("dp", "seq", "tensor"),
        P("dp", "seq", "tensor"),
        P("dp", "seq", "tensor"),
        P("dp", "seq", "tensor"),
        P("tensor", ("dp", "seq")),
    )
    return jax.shard_map(shards_body, mesh=mesh, in_specs=in_specs, out_specs=out_specs, check_vma=False)
```
